256 devices in a mesh: grp: 8 (over z_lo, y), tile: 32 (over z_hi, x, core).
Axes of the slice: x: 4, y: 4, z: 8 (z_hi: 4, z_lo: 2; z = z_hi * 2 + z_lo), core: 2. Of those that a mesh axis runs over, the one named last changes fastest.
Arguments:
- parent_state: float32 [3, 8, 2048, 2048], P(None, None, ('grp', 'tile')), may hold values from -6 to 6
- terrain: int32 [2048, 2048], P(('grp', 'tile')), may hold values from 0 to 4000
- nest_state: float32 [3, 8, 8, 384, 768], P(None, None, 'grp', 'tile'), may hold values from -6 to 6
- nest_offsets: int32 [8, 2], P('grp'), may hold values from 1 to 1791, as said below
Outputs:
- new_parent: float32 [3, 8, 2048, 2048], P(None, None, ('grp', 'tile'))
- new_nest: float32 [3, 8, 8, 384, 768], P(None, None, 'grp', 'tile')
The draws below stay inside these ranges and needn't reach their ends.
Inputs may be any that keep to these rules, and one draw needn't show every extreme that they name: `nest_offsets`: row g holds nest g's first footprint row counted within group g's band of 256 parent rows, from 1 to 127, and its first footprint column, from 1 to 1791. In every draw one nest has the largest row offset and column offset 1, and another nest has the largest column offset.
All inputs are finite; a program needn't handle non-finite values.
Results may differ from the reference program's by a relative error of at most 0.0001.
Values sent between devices are 32-bit elements; how exact they have to be, the bound alone decides.
No kernel may reach another device: no remote copies, remote signals or barrier semaphores. Data moves between devices by JAX's collectives and lax.ppermute only.
A program may use at most 128 MiB of HBM per device.

```python
import jax
import jax.numpy as jnp
from jax import lax

PR = 2048
PC = 2048
NC = 768
LEV = 8
NRD = 12
SUBSTEPS = 3
BAND = 256
NEST = 8
NR = 384
N_GRP = 8
N_TILE = 32


def draw_nest_offsets(key, part):
    key_rows, key_cols, key_first, key_second = jax.random.split(jax.random.fold_in(key, 11), 4)
    row_top = PR // N_GRP - NRD * N_TILE // 3 - 1
    col_top = PC - NC // 3 - 1
    row_values = jax.random.randint(key_rows, (NEST,), 1, row_top + 1)
    col_values = jax.random.randint(key_cols, (NEST,), 1, col_top + 1)
    first_nest = jax.random.randint(key_first, (), 0, NEST)
    second_nest = (first_nest + 1 + jax.random.randint(key_second, (), 0, NEST - 1)) % NEST
    row_values = row_values.at[first_nest].set(row_top)
    col_values = col_values.at[first_nest].set(1).at[second_nest].set(col_top)
    return jnp.stack([row_values, col_values], axis=1).astype(jnp.int32)


def place_ends(values, own_key, low, high):
    dims = values.shape
    index_at = [jax.random.randint(jax.random.fold_in(own_key, axis), (), 0, dims[axis]) for axis in range(len(dims))]
    values = values.at[tuple(index_at)].set(low)
    longest = dims.index(max(dims))
    index_at[longest] = (index_at[longest] + 1) % dims[longest]
    return values.at[tuple(index_at)].set(high)


def level_of(key, shape, pieces, smallest, high):
    gain = 1.0
    for position, shards_of in pieces:
        heights = jax.random.uniform(jax.random.fold_in(jax.random.fold_in(key, 6), position), (shards_of,), jnp.float32, smallest / len(pieces), high / len(pieces))
        gain = gain * jnp.repeat(jnp.exp(heights), shape[position] // shards_of).reshape((-1,) + (1,) * (len(shape) - 1 - position))
    return gain


def gaussian(stream_key, shape, spread, reach, cuts=(), kind=jnp.bfloat16):
    gain = level_of(stream_key, shape, cuts, -0.22, 0.18) if cuts else 1.0
    values = jax.random.normal(stream_key, shape, jnp.float32) * spread * gain
    return jnp.minimum(jnp.maximum(values, -reach), reach).astype(kind)


def setup_inputs(seed: int = 0) -> dict:
    arg_keys = jax.random.split(jax.random.key(seed), 5)
    parent_state = gaussian(arg_keys[0], (3, LEV, PR, PC), 1.0, 6.0, ((2, 256),), jnp.float32)
    terrain = place_ends(jax.random.randint(arg_keys[1], (PR, PC), 0, 4001), jax.random.fold_in(arg_keys[1], 1), 0, 4000).astype(jnp.int32)
    nest_state = gaussian(arg_keys[2], (3, LEV, NEST, NR, NC), 1.0, 6.0, ((2, 8), (3, 32)), jnp.float32)
    nest_offsets = draw_nest_offsets(jax.random.fold_in(arg_keys[4], 71), 0)
    return {"parent_state": parent_state, "terrain": terrain, "nest_state": nest_state, "nest_offsets": nest_offsets}


parent_courant = 0.35
nest_courant = 0.35
nudge_rate = 0.2
terrain_scale = 6000.0


def substep(fields, sound_factor, courant, east_edge, west_edge):
    pressure = fields[0]
    zonal_wind = fields[1]
    merid_wind = fields[2]
    east_side = jnp.concatenate([pressure[..., 1:], east_edge[..., None]], axis=-1)
    zonal_next = zonal_wind - courant * (east_side - pressure)
    below_side = jnp.concatenate([pressure[..., 1:, :], jnp.zeros_like(pressure[..., :1, :])], axis=-2)
    merid_next = merid_wind - courant * (below_side - pressure)
    west_side = jnp.concatenate([west_edge[..., None], zonal_next[..., :-1]], axis=-1)
    above_side = jnp.concatenate([jnp.zeros_like(merid_next[..., :1, :]), merid_next[..., :-1, :]], axis=-2)
    pressure_next = pressure - courant * sound_factor * ((zonal_next - west_side) + (merid_next - above_side))
    return jnp.stack([pressure_next, zonal_next, merid_next])


def reference(parent_state, terrain, nest_state, nest_offsets):
    sound_factor = 1.0 - terrain.astype(jnp.float32) / terrain_scale
    factor_ext = jnp.pad(sound_factor, ((1, 1), (0, 0)))
    edge_zeros = jnp.zeros((PR + 2,), jnp.float32)

    def one_level(level_fields):
        extended = jnp.pad(level_fields, ((0, 0), (1, 1), (0, 0)))
        return substep(extended, factor_ext, parent_courant, edge_zeros, edge_zeros)[:, 1:-1, :]

    advanced = jnp.moveaxis(lax.map(one_level, jnp.moveaxis(parent_state, 1, 0)), 0, 1)
    result = advanced
    coarse_rows = NR // 3
    coarse_cols = NC // 3
    zero_index = jnp.zeros((), jnp.int32)
    nest_list = []
    for nest_index in range(NEST):
        row_start = (nest_index * BAND + nest_offsets[nest_index, 0]).astype(jnp.int32)
        col_start = nest_offsets[nest_index, 1].astype(jnp.int32)
        footprint = lax.dynamic_slice(advanced, (zero_index, zero_index, row_start - 1, col_start - 1),
                                      (3, LEV, coarse_rows + 2, coarse_cols + 2))
        foot_factor = lax.dynamic_slice(sound_factor, (row_start - 1, col_start - 1),
                                        (coarse_rows + 2, coarse_cols + 2))
        injected = jnp.repeat(jnp.repeat(footprint[..., 1:-1], 3, axis=3), 3, axis=2)[:, :, 2:-2]
        west_rows = jnp.repeat(footprint[1, :, :, 0], 3, axis=1)[:, 2:-2]
        east_rows = jnp.repeat(footprint[0, :, :, -1], 3, axis=1)[:, 2:-2]
        factor_rows = jnp.repeat(jnp.repeat(foot_factor[:, 1:-1], 3, axis=1), 3, axis=0)[2:-2]
        fields = nest_state[:, :, nest_index]
        for _ in range(SUBSTEPS):
            extended = jnp.concatenate([injected[:, :, :1], fields, injected[:, :, -1:]], axis=2)
            stepped = substep(extended, factor_rows, nest_courant, east_rows, west_rows)
            fields = (stepped + nudge_rate * (injected - stepped))[:, :, 1:-1]
        nest_list.append(fields)
        block_means = fields.reshape(3, LEV, coarse_rows, 3, coarse_cols, 3).mean(axis=(3, 5))
        result = lax.dynamic_update_slice(result, block_means, (zero_index, zero_index, row_start, col_start))
    return result, jnp.stack(nest_list, axis=2)
```

```python
import jax
import jax.numpy as jnp
from jax import lax
from jax.sharding import PartitionSpec as P

SUBSTEPS = 3


parent_courant = 0.35
nest_courant = 0.35
nudge_rate = 0.2
terrain_scale = 6000.0

HIGHEST = lax.Precision.HIGHEST


def shift_from(value, axis, offset, devices):
    pairs = [(d + offset, d) for d in range(devices) if 0 <= d + offset < devices]
    return lax.ppermute(value, axis, pairs)


def extended_2(value, sides, width):
    for axis, dim in sides:
        devices, length = (lax.axis_size(axis), value.shape[dim])
        up = [(i, (i + 1) % devices) for i in range(devices - 1)]
        down = [(j, i) for i, j in up]
        last = lax.slice_in_dim(value, length - width, length, axis=dim)
        first = lax.slice_in_dim(value, 0, width, axis=dim)
        before = lax.ppermute(last, axis, up)
        after = lax.ppermute(first, axis, down)
        value = jnp.concatenate([before, value, after], axis=dim)
    return value


def substep(fields, sound_factor, courant, east_edge, west_edge):
    pressure = fields[0]
    zonal_wind = fields[1]
    merid_wind = fields[2]
    east_side = jnp.concatenate([pressure[..., 1:], east_edge[..., None]], axis=-1)
    zonal_next = zonal_wind - courant * (east_side - pressure)
    below_side = jnp.concatenate(
        [pressure[..., 1:, :], jnp.zeros_like(pressure[..., :1, :])], axis=-2
    )
    merid_next = merid_wind - courant * (below_side - pressure)
    west_side = jnp.concatenate([west_edge[..., None], zonal_next[..., :-1]], axis=-1)
    above_side = jnp.concatenate(
        [jnp.zeros_like(merid_next[..., :1, :]), merid_next[..., :-1, :]], axis=-2
    )
    pressure_next = pressure - courant * sound_factor * (
        zonal_next - west_side + (merid_next - above_side)
    )
    return jnp.stack([pressure_next, zonal_next, merid_next])


def repeat_matrix(small, factor):
    rows = jnp.arange(small, dtype=jnp.int32)[:, None]
    cols = jnp.arange(small * factor, dtype=jnp.int32)[None, :] // factor
    return (rows == cols).astype(jnp.float32)


def local(parent_state, terrain, nest_state, nest_offsets):
    tiles = lax.axis_size("tile")
    tile_index = lax.axis_index("tile")
    levels = parent_state.shape[1]
    parent_rows = parent_state.shape[2]
    nest_rows = nest_state.shape[3]
    nest_cols = nest_state.shape[4]
    coarse_rows = nest_rows // 3
    coarse_cols = nest_cols // 3
    foot_rows = coarse_rows + 2
    assert parent_rows == 2 * coarse_rows
    band_rows = parent_rows * tiles
    nest_total = nest_rows * tiles
    coarse_total = nest_total // 3
    largest_offset = band_rows - coarse_total - 1
    largest_q = largest_offset // parent_rows
    bits = max(1, int(largest_q).bit_length())
    planes = 3 * levels

    row_offset = nest_offsets[0, 0]
    col_offset = nest_offsets[0, 1]
    q = row_offset // parent_rows
    r = row_offset - q * parent_rows

    nest_fields = nest_state[:, :, 0]
    above3 = shift_from(nest_fields[:, :, nest_rows - 3 :], "tile", -1, tiles)
    below3 = shift_from(nest_fields[:, :, :3], "tile", 1, tiles)

    sound_factor = 1.0 - terrain.astype(jnp.float32) / terrain_scale
    halo_fields = parent_state[0:3:2]
    padded = extended_2(halo_fields, ((("grp", "tile"), 2),), 1)
    zonal_ext = jnp.pad(parent_state[1], ((0, 0), (1, 1), (0, 0)))
    extended = jnp.stack([padded[0], zonal_ext, padded[1]])
    factor_ext = jnp.pad(sound_factor, ((1, 1), (0, 0)))
    edge_zeros = jnp.zeros((levels, parent_rows + 2), jnp.float32)
    advanced = substep(extended, factor_ext, parent_courant, edge_zeros, edge_zeros)[:, :, 1:-1]

    window = lax.dynamic_slice_in_dim(advanced, col_offset - 1, coarse_cols + 2, axis=3)
    factor_window = lax.dynamic_slice_in_dim(sound_factor, col_offset - 1, coarse_cols + 2, axis=1)
    rows_here = jnp.concatenate(
        [window.reshape(planes, parent_rows, coarse_cols + 2), factor_window[None]], axis=0
    )
    last_before = shift_from(rows_here[:, parent_rows - 1 :], "tile", -1, tiles)
    rows_after = shift_from(rows_here, "tile", 1, tiles)
    joined = jnp.concatenate([last_before, rows_here, rows_after], axis=1)
    block = lax.dynamic_slice_in_dim(joined, r, parent_rows + 2, axis=1)
    for k in range(bits):
        moved = shift_from(block, "tile", 1 << k, tiles)
        block = jnp.where(((q >> k) & 1) == 1, moved, block)
    half = tiles // 2
    to_even = lax.ppermute(block[:, 0:foot_rows], "tile", [(m, 2 * m) for m in range(half)])
    to_odd = lax.ppermute(
        block[:, coarse_rows : coarse_rows + foot_rows], "tile", [(m, 2 * m + 1) for m in range(half)]
    )
    footprint = jnp.where(tile_index % 2 == 0, to_even, to_odd)

    widen = repeat_matrix(coarse_cols, 3)
    heighten = repeat_matrix(foot_rows, 3).T
    inner = jnp.einsum("pic,cj->pij", footprint[:, :, 1:-1], widen, precision=HIGHEST)
    expanded = jnp.einsum("ri,pij->prj", heighten, inner, precision=HIGHEST)
    injected = expanded[:planes].reshape(3, levels, 3 * foot_rows, nest_cols)
    nest_factor = expanded[planes]
    west_rows = jnp.repeat(footprint[levels : 2 * levels, :, 0], 3, axis=1)
    east_rows = jnp.repeat(footprint[0:levels, :, -1], 3, axis=1)

    local_rows = jnp.arange(3 * foot_rows, dtype=jnp.int32) - 3
    global_rows = nest_rows * tile_index + local_rows
    outside = ((global_rows < 0) | (global_rows >= nest_total))[None, None, :, None]
    fields = jnp.concatenate([above3, nest_fields, below3], axis=2)
    for _ in range(SUBSTEPS):
        fields = jnp.where(outside, injected, fields)
        stepped = substep(fields, nest_factor, nest_courant, east_rows, west_rows)
        fields = stepped + nudge_rate * (injected - stepped)
    new_nest = fields[:, :, 3 : 3 + nest_rows]

    narrow = repeat_matrix(coarse_cols, 3).T
    shorten = repeat_matrix(coarse_rows, 3)
    col_sums = jnp.einsum("plrj,jc->plrc", new_nest, narrow, precision=HIGHEST)
    sums = jnp.einsum("kr,plrc->plkc", shorten, col_sums, precision=HIGHEST)
    means = (sums / 9.0).reshape(planes, coarse_rows, coarse_cols)

    from_even = lax.ppermute(means, "tile", [(2 * m, m) for m in range(half)])
    from_odd = lax.ppermute(means, "tile", [(2 * m + 1, m) for m in range(half)])
    back = jnp.concatenate([from_even, from_odd], axis=1)
    for k in range(bits):
        moved = shift_from(back, "tile", -(1 << k), tiles)
        back = jnp.where(((q >> k) & 1) == 1, moved, back)
    back_before = shift_from(back, "tile", -1, tiles)
    both = jnp.concatenate([back_before, back], axis=1)
    placed = lax.dynamic_slice_in_dim(both, parent_rows - r, parent_rows, axis=1)
    placed = placed.reshape(3, levels, parent_rows, coarse_cols)
    band_row = parent_rows * tile_index + jnp.arange(parent_rows, dtype=jnp.int32) - row_offset
    covered = ((band_row >= 0) & (band_row < coarse_total))[None, None, :, None]
    previous = lax.dynamic_slice_in_dim(advanced, col_offset, coarse_cols, axis=3)
    merged = jnp.where(covered, placed, previous)
    new_parent = lax.dynamic_update_slice_in_dim(advanced, merged, col_offset, axis=3)
    return (new_parent, new_nest[:, :, None])


def solution(mesh):
    placed = (
        P(None, None, ("grp", "tile"), None),
        P(("grp", "tile"), None),
        P(None, None, "grp", "tile", None),
        P("grp", None),
    )
    return jax.shard_map(
        local,
        mesh=mesh,
        in_specs=placed,
        out_specs=(P(None, None, ("grp", "tile"), None), P(None, None, "grp", "tile", None)),
        check_vma=False,
    )
```

```python
import jax
import jax.numpy as jnp
from jax import lax
from jax.sharding import PartitionSpec as P

SUBSTEPS = 3


parent_courant = 0.35
nest_courant = 0.35
nudge_rate = 0.2
terrain_scale = 6000.0

HIGHEST = lax.Precision.HIGHEST


def shift_from(value, axis, offset, devices):
    pairs = [(d + offset, d) for d in range(devices) if 0 <= d + offset < devices]
    return lax.ppermute(value, axis, pairs)


def extended_2(value, sides, width):
    for axis, dim in sides:
        devices, length = (lax.axis_size(axis), value.shape[dim])
        up = [(i, (i + 1) % devices) for i in range(devices - 1)]
        down = [(j, i) for i, j in up]
        last = lax.slice_in_dim(value, length - width, length, axis=dim)
        first = lax.slice_in_dim(value, 0, width, axis=dim)
        before = lax.ppermute(last, axis, up)
        after = lax.ppermute(first, axis, down)
        value = jnp.concatenate([before, value, after], axis=dim)
    return value


def substep(fields, sound_factor, courant, east_edge, west_edge):
    pressure = fields[0]
    zonal_wind = fields[1]
    merid_wind = fields[2]
    east_side = jnp.concatenate([pressure[..., 1:], east_edge[..., None]], axis=-1)
    zonal_next = zonal_wind - courant * (east_side - pressure)
    below_side = jnp.concatenate(
        [pressure[..., 1:, :], jnp.zeros_like(pressure[..., :1, :])], axis=-2
    )
    merid_next = merid_wind - courant * (below_side - pressure)
    west_side = jnp.concatenate([west_edge[..., None], zonal_next[..., :-1]], axis=-1)
    above_side = jnp.concatenate(
        [jnp.zeros_like(merid_next[..., :1, :]), merid_next[..., :-1, :]], axis=-2
    )
    pressure_next = pressure - courant * sound_factor * (
        zonal_next - west_side + (merid_next - above_side)
    )
    return jnp.stack([pressure_next, zonal_next, merid_next])


def repeat_matrix(small, factor):
    rows = jnp.arange(small, dtype=jnp.int32)[:, None]
    cols = jnp.arange(small * factor, dtype=jnp.int32)[None, :] // factor
    return (rows == cols).astype(jnp.float32)


def barrel(value, amount, digits, direction, tiles):
    for j in range(digits):
        digit = (amount >> (2 * j)) & 3
        step = 4**j
        moved = [shift_from(value, "tile", direction * k * step, tiles) for k in (1, 2, 3)]
        value = jnp.where(
            digit == 0, value, jnp.where(digit == 1, moved[0], jnp.where(digit == 2, moved[1], moved[2]))
        )
    return value


def local(parent_state, terrain, nest_state, nest_offsets):
    tiles = lax.axis_size("tile")
    tile_index = lax.axis_index("tile")
    levels = parent_state.shape[1]
    parent_rows = parent_state.shape[2]
    nest_rows = nest_state.shape[3]
    nest_cols = nest_state.shape[4]
    coarse_rows = nest_rows // 3
    coarse_cols = nest_cols // 3
    foot_rows = coarse_rows + 2
    assert parent_rows == 2 * coarse_rows and 2 * levels <= coarse_cols
    band_rows = parent_rows * tiles
    nest_total = nest_rows * tiles
    coarse_total = nest_total // 3
    largest_offset = band_rows - coarse_total - 1
    largest_q = largest_offset // parent_rows
    digits = max(1, (int(largest_q).bit_length() + 1) // 2)
    planes = 3 * levels
    half = tiles // 2

    row_offset = nest_offsets[0, 0]
    col_offset = nest_offsets[0, 1]
    q = row_offset // parent_rows
    r = row_offset - q * parent_rows

    nest_fields = nest_state[:, :, 0]
    above3 = shift_from(nest_fields[:, :, nest_rows - 3 :], "tile", -1, tiles)
    below3 = shift_from(nest_fields[:, :, :3], "tile", 1, tiles)

    sound_factor = 1.0 - terrain.astype(jnp.float32) / terrain_scale
    halo_fields = parent_state[0:3:2]
    padded = extended_2(halo_fields, ((("grp", "tile"), 2),), 1)
    zonal_ext = jnp.pad(parent_state[1], ((0, 0), (1, 1), (0, 0)))
    extended = jnp.stack([padded[0], zonal_ext, padded[1]])
    factor_ext = jnp.pad(sound_factor, ((1, 1), (0, 0)))
    edge_zeros = jnp.zeros((levels, parent_rows + 2), jnp.float32)
    advanced = substep(extended, factor_ext, parent_courant, edge_zeros, edge_zeros)[:, :, 1:-1]

    window = lax.dynamic_slice_in_dim(advanced, col_offset - 1, coarse_cols + 2, axis=3)
    factor_window = lax.dynamic_slice_in_dim(sound_factor, col_offset, coarse_cols, axis=1)
    east_col = window[0, :, :, -1].T
    west_col = window[1, :, :, 0].T
    edge_plane = jnp.concatenate(
        [east_col, west_col, jnp.zeros((parent_rows, coarse_cols - 2 * levels), jnp.float32)], axis=1
    )
    rows_here = jnp.concatenate(
        [
            window[..., 1:-1].reshape(planes, parent_rows, coarse_cols),
            factor_window[None],
            edge_plane[None],
        ],
        axis=0,
    )
    above3, below3, rows_here = lax.optimization_barrier((above3, below3, rows_here))
    last_before = shift_from(rows_here[:, parent_rows - 1], "tile", -1, tiles)
    rows_after = shift_from(rows_here, "tile", 1, tiles)
    joined = jnp.concatenate([last_before[:, None], rows_here, rows_after], axis=1)
    block = lax.dynamic_slice_in_dim(joined, r, parent_rows, axis=1)
    block = barrel(block, q, digits, 1, tiles)
    to_even = lax.ppermute(block, "tile", [(m, 2 * m) for m in range(half)])
    to_odd = lax.ppermute(block, "tile", [(m, 2 * m + 1) for m in range(half)])
    next_odd = lax.ppermute(block, "tile", [(m + 1, 2 * m + 1) for m in range(half)])
    odd_rows = jnp.concatenate([to_odd[:, coarse_rows:], next_odd[:, : foot_rows - coarse_rows]], axis=1)
    footprint = jnp.where(tile_index % 2 == 0, to_even[:, :foot_rows], odd_rows)

    widen = repeat_matrix(coarse_cols, 3)
    heighten = repeat_matrix(foot_rows, 3).T
    inner = jnp.einsum("pic,cj->pij", footprint[: planes + 1], widen, precision=HIGHEST)
    expanded = jnp.einsum("ri,pij->prj", heighten, inner, precision=HIGHEST)
    injected = expanded[:planes].reshape(3, levels, 3 * foot_rows, nest_cols)
    nest_factor = expanded[planes]
    east_rows = jnp.repeat(footprint[planes + 1, :, 0:levels].T, 3, axis=1)
    west_rows = jnp.repeat(footprint[planes + 1, :, levels : 2 * levels].T, 3, axis=1)

    local_rows = jnp.arange(3 * foot_rows, dtype=jnp.int32) - 3
    global_rows = nest_rows * tile_index + local_rows
    outside = ((global_rows < 0) | (global_rows >= nest_total))[None, None, :, None]
    fields = jnp.concatenate([above3, nest_fields, below3], axis=2)
    for _ in range(SUBSTEPS):
        fields = jnp.where(outside, injected, fields)
        stepped = substep(fields, nest_factor, nest_courant, east_rows, west_rows)
        fields = stepped + nudge_rate * (injected - stepped)
    new_nest = fields[:, :, 3 : 3 + nest_rows]

    narrow = repeat_matrix(coarse_cols, 3).T
    shorten = repeat_matrix(coarse_rows, 3)
    col_sums = jnp.einsum("plrj,jc->plrc", new_nest, narrow, precision=HIGHEST)
    sums = jnp.einsum("kr,plrc->kplc", shorten, col_sums, precision=HIGHEST)
    means = (sums / 9.0).reshape(coarse_rows, planes, coarse_cols)

    gathered = [
        lax.ppermute(means, "tile", [(2 * m + k, m) for m in range(half + 1) if 0 <= 2 * m + k < tiles])
        for k in (-2, -1, 0, 1)
    ]
    both = jnp.concatenate(gathered, axis=0)
    back = lax.dynamic_slice_in_dim(both, parent_rows - r, parent_rows, axis=0)
    back = barrel(back, q, digits, -1, tiles)
    placed = jnp.transpose(back, (1, 0, 2)).reshape(3, levels, parent_rows, coarse_cols)
    band_row = parent_rows * tile_index + jnp.arange(parent_rows, dtype=jnp.int32) - row_offset
    covered = ((band_row >= 0) & (band_row < coarse_total))[None, None, :, None]
    previous = lax.dynamic_slice_in_dim(advanced, col_offset, coarse_cols, axis=3)
    merged = jnp.where(covered, placed, previous)
    new_parent = lax.dynamic_update_slice_in_dim(advanced, merged, col_offset, axis=3)
    return (new_parent, new_nest[:, :, None])


def solution(mesh):
    placed = (
        P(None, None, ("grp", "tile"), None),
        P(("grp", "tile"), None),
        P(None, None, "grp", "tile", None),
        P("grp", None),
    )
    return jax.shard_map(
        local,
        mesh=mesh,
        in_specs=placed,
        out_specs=(P(None, None, ("grp", "tile"), None), P(None, None, "grp", "tile", None)),
        check_vma=False,
    )
```

```python
import jax
import jax.numpy as jnp
from jax import lax
from jax.sharding import PartitionSpec as P

SUBSTEPS = 3


parent_courant = 0.35
nest_courant = 0.35
nudge_rate = 0.2
terrain_scale = 6000.0

HIGHEST = lax.Precision.HIGHEST


def shift_from(value, axis, offset, devices):
    pairs = [(d + offset, d) for d in range(devices) if 0 <= d + offset < devices]
    return lax.ppermute(value, axis, pairs)


def extended_2(value, sides, width):
    for axis, dim in sides:
        devices, length = (lax.axis_size(axis), value.shape[dim])
        up = [(i, (i + 1) % devices) for i in range(devices - 1)]
        down = [(j, i) for i, j in up]
        last = lax.slice_in_dim(value, length - width, length, axis=dim)
        first = lax.slice_in_dim(value, 0, width, axis=dim)
        before = lax.ppermute(last, axis, up)
        after = lax.ppermute(first, axis, down)
        value = jnp.concatenate([before, value, after], axis=dim)
    return value


def substep(fields, sound_factor, courant, east_edge, west_edge):
    pressure = fields[0]
    zonal_wind = fields[1]
    merid_wind = fields[2]
    east_side = jnp.concatenate([pressure[..., 1:], east_edge[..., None]], axis=-1)
    zonal_next = zonal_wind - courant * (east_side - pressure)
    below_side = jnp.concatenate(
        [pressure[..., 1:, :], jnp.zeros_like(pressure[..., :1, :])], axis=-2
    )
    merid_next = merid_wind - courant * (below_side - pressure)
    west_side = jnp.concatenate([west_edge[..., None], zonal_next[..., :-1]], axis=-1)
    above_side = jnp.concatenate(
        [jnp.zeros_like(merid_next[..., :1, :]), merid_next[..., :-1, :]], axis=-2
    )
    pressure_next = pressure - courant * sound_factor * (
        zonal_next - west_side + (merid_next - above_side)
    )
    return jnp.stack([pressure_next, zonal_next, merid_next])


def repeat_matrix(small, factor):
    rows = jnp.arange(small, dtype=jnp.int32)[:, None]
    cols = jnp.arange(small * factor, dtype=jnp.int32)[None, :] // factor
    return (rows == cols).astype(jnp.float32)


def pick(value, options, tiles):
    out = value
    for offset, predicate in options:
        out = jnp.where(predicate, shift_from(value, "tile", offset, tiles), out)
    return out


def local(parent_state, terrain, nest_state, nest_offsets):
    tiles = lax.axis_size("tile")
    tile_index = lax.axis_index("tile")
    levels = parent_state.shape[1]
    parent_rows = parent_state.shape[2]
    nest_rows = nest_state.shape[3]
    nest_cols = nest_state.shape[4]
    coarse_rows = nest_rows // 3
    coarse_cols = nest_cols // 3
    foot_rows = coarse_rows + 2
    assert parent_rows == 2 * coarse_rows and 2 * levels <= coarse_cols
    band_rows = parent_rows * tiles
    nest_total = nest_rows * tiles
    coarse_total = nest_total // 3
    largest_offset = band_rows - coarse_total - 1
    largest_q = largest_offset // parent_rows
    assert largest_q < 16 and tiles >= 2 * 16
    center = 8
    planes = 3 * levels
    half = tiles // 2

    row_offset = nest_offsets[0, 0]
    col_offset = nest_offsets[0, 1]
    q = row_offset // parent_rows
    r = row_offset - q * parent_rows

    nest_fields = nest_state[:, :, 0]
    above3 = shift_from(nest_fields[:, :, nest_rows - 3 :], "tile", -1, tiles)
    below3 = shift_from(nest_fields[:, :, :3], "tile", 1, tiles)

    sound_factor = 1.0 - terrain.astype(jnp.float32) / terrain_scale
    halo_fields = parent_state[0:3:2]
    padded = extended_2(halo_fields, ((("grp", "tile"), 2),), 1)
    zonal_ext = jnp.pad(parent_state[1], ((0, 0), (1, 1), (0, 0)))
    extended = jnp.stack([padded[0], zonal_ext, padded[1]])
    factor_ext = jnp.pad(sound_factor, ((1, 1), (0, 0)))
    edge_zeros = jnp.zeros((levels, parent_rows + 2), jnp.float32)
    advanced = substep(extended, factor_ext, parent_courant, edge_zeros, edge_zeros)[:, :, 1:-1]

    window = lax.dynamic_slice_in_dim(advanced, col_offset - 1, coarse_cols + 2, axis=3)
    factor_window = lax.dynamic_slice_in_dim(sound_factor, col_offset, coarse_cols, axis=1)
    east_col = window[0, :, :, -1].T
    west_col = window[1, :, :, 0].T
    edge_plane = jnp.concatenate(
        [east_col, west_col, jnp.zeros((parent_rows, coarse_cols - 2 * levels), jnp.float32)], axis=1
    )
    rows_here = jnp.concatenate(
        [
            window[..., 1:-1].reshape(planes, parent_rows, coarse_cols),
            factor_window[None],
            edge_plane[None],
        ],
        axis=0,
    )
    above3, below3, rows_here = lax.optimization_barrier((above3, below3, rows_here))
    last_before = shift_from(rows_here[:, parent_rows - 1], "tile", -1, tiles)
    rows_after = shift_from(rows_here, "tile", 1, tiles)
    joined = jnp.concatenate([last_before[:, None], rows_here, rows_after], axis=1)
    block = lax.dynamic_slice_in_dim(joined, r, parent_rows, axis=1)
    low = q & 3
    bit2 = ((q >> 2) & 1) == 1
    bit3 = ((q >> 3) & 1) == 1
    block = pick(block, [(1, low == 1), (2, low == 2), (3, low == 3)], tiles)
    block = pick(block, [(4, bit2)], tiles)
    block = pick(block, [(-center, jnp.logical_not(bit3))], tiles)
    to_even = lax.ppermute(block, "tile", [(m + center, 2 * m) for m in range(half)])
    to_odd = lax.ppermute(block, "tile", [(m + center, 2 * m + 1) for m in range(half)])
    next_odd = lax.ppermute(block, "tile", [(m + center + 1, 2 * m + 1) for m in range(half)])
    odd_rows = jnp.concatenate([to_odd[:, coarse_rows:], next_odd[:, : foot_rows - coarse_rows]], axis=1)
    footprint = jnp.where(tile_index % 2 == 0, to_even[:, :foot_rows], odd_rows)

    widen = repeat_matrix(coarse_cols, 3)
    heighten = repeat_matrix(foot_rows, 3).T
    inner = jnp.einsum("pic,cj->pij", footprint[: planes + 1], widen, precision=HIGHEST)
    expanded = jnp.einsum("ri,pij->prj", heighten, inner, precision=HIGHEST)
    injected = expanded[:planes].reshape(3, levels, 3 * foot_rows, nest_cols)
    nest_factor = expanded[planes]
    east_rows = jnp.repeat(footprint[planes + 1, :, 0:levels].T, 3, axis=1)
    west_rows = jnp.repeat(footprint[planes + 1, :, levels : 2 * levels].T, 3, axis=1)

    local_rows = jnp.arange(3 * foot_rows, dtype=jnp.int32) - 3
    global_rows = nest_rows * tile_index + local_rows
    outside = ((global_rows < 0) | (global_rows >= nest_total))[None, None, :, None]
    fields = jnp.concatenate([above3, nest_fields, below3], axis=2)
    for _ in range(SUBSTEPS):
        fields = jnp.where(outside, injected, fields)
        stepped = substep(fields, nest_factor, nest_courant, east_rows, west_rows)
        fields = stepped + nudge_rate * (injected - stepped)
    new_nest = fields[:, :, 3 : 3 + nest_rows]

    narrow = repeat_matrix(coarse_cols, 3).T
    shorten = repeat_matrix(coarse_rows, 3)
    col_sums = jnp.einsum("plrj,jc->plrc", new_nest, narrow, precision=HIGHEST)
    sums = jnp.einsum("kr,plrc->kplc", shorten, col_sums, precision=HIGHEST)
    means = (sums / 9.0).reshape(coarse_rows, planes, coarse_cols)

    gathered = [
        lax.ppermute(
            means, "tile", [(2 * m + k, m + center) for m in range(half + 1) if 0 <= 2 * m + k < tiles]
        )
        for k in (-2, -1, 0, 1)
    ]
    both = jnp.concatenate(gathered, axis=0)
    back = lax.dynamic_slice_in_dim(both, parent_rows - r, parent_rows, axis=0)
    back = pick(back, [(center, jnp.logical_not(bit3))], tiles)
    back = pick(back, [(-1, low == 1), (-2, low == 2), (-3, low == 3)], tiles)
    back = pick(back, [(-4, bit2)], tiles)
    placed = jnp.transpose(back, (1, 0, 2)).reshape(3, levels, parent_rows, coarse_cols)
    band_row = parent_rows * tile_index + jnp.arange(parent_rows, dtype=jnp.int32) - row_offset
    covered = ((band_row >= 0) & (band_row < coarse_total))[None, None, :, None]
    previous = lax.dynamic_slice_in_dim(advanced, col_offset, coarse_cols, axis=3)
    merged = jnp.where(covered, placed, previous)
    new_parent = lax.dynamic_update_slice_in_dim(advanced, merged, col_offset, axis=3)
    return (new_parent, new_nest[:, :, None])


def solution(mesh):
    placed = (
        P(None, None, ("grp", "tile"), None),
        P(("grp", "tile"), None),
        P(None, None, "grp", "tile", None),
        P("grp", None),
    )
    return jax.shard_map(
        local,
        mesh=mesh,
        in_specs=placed,
        out_specs=(P(None, None, ("grp", "tile"), None), P(None, None, "grp", "tile", None)),
        check_vma=False,
    )
```

```python
import jax
import jax.numpy as jnp
from jax import lax
from jax.sharding import PartitionSpec as P

SUBSTEPS = 3


parent_courant = 0.35
nest_courant = 0.35
nudge_rate = 0.2
terrain_scale = 6000.0

HIGHEST = lax.Precision.HIGHEST


def shift_from(value, axis, offset, devices):
    pairs = [(d + offset, d) for d in range(devices) if 0 <= d + offset < devices]
    return lax.ppermute(value, axis, pairs)


def extended_2(value, sides, width):
    for axis, dim in sides:
        devices, length = (lax.axis_size(axis), value.shape[dim])
        up = [(i, (i + 1) % devices) for i in range(devices - 1)]
        down = [(j, i) for i, j in up]
        last = lax.slice_in_dim(value, length - width, length, axis=dim)
        first = lax.slice_in_dim(value, 0, width, axis=dim)
        before = lax.ppermute(last, axis, up)
        after = lax.ppermute(first, axis, down)
        value = jnp.concatenate([before, value, after], axis=dim)
    return value


def substep(fields, sound_factor, courant, east_edge, west_edge):
    pressure = fields[0]
    zonal_wind = fields[1]
    merid_wind = fields[2]
    east_side = jnp.concatenate([pressure[..., 1:], east_edge[..., None]], axis=-1)
    zonal_next = zonal_wind - courant * (east_side - pressure)
    below_side = jnp.concatenate(
        [pressure[..., 1:, :], jnp.zeros_like(pressure[..., :1, :])], axis=-2
    )
    merid_next = merid_wind - courant * (below_side - pressure)
    west_side = jnp.concatenate([west_edge[..., None], zonal_next[..., :-1]], axis=-1)
    above_side = jnp.concatenate(
        [jnp.zeros_like(merid_next[..., :1, :]), merid_next[..., :-1, :]], axis=-2
    )
    pressure_next = pressure - courant * sound_factor * (
        zonal_next - west_side + (merid_next - above_side)
    )
    return jnp.stack([pressure_next, zonal_next, merid_next])


def repeat_matrix(small, factor):
    rows = jnp.arange(small, dtype=jnp.int32)[:, None]
    cols = jnp.arange(small * factor, dtype=jnp.int32)[None, :] // factor
    return (rows == cols).astype(jnp.float32)


def pick(value, options, tiles):
    out = value
    for offset, predicate in options:
        out = jnp.where(predicate, shift_from(value, "tile", offset, tiles), out)
    return out


def local(parent_state, terrain, nest_state, nest_offsets):
    tiles = lax.axis_size("tile")
    tile_index = lax.axis_index("tile")
    levels = parent_state.shape[1]
    parent_rows = parent_state.shape[2]
    nest_rows = nest_state.shape[3]
    nest_cols = nest_state.shape[4]
    coarse_rows = nest_rows // 3
    coarse_cols = nest_cols // 3
    foot_rows = coarse_rows + 2
    assert parent_rows == 2 * coarse_rows and 2 * levels <= coarse_cols
    band_rows = parent_rows * tiles
    nest_total = nest_rows * tiles
    coarse_total = nest_total // 3
    largest_offset = band_rows - coarse_total - 1
    largest_q = largest_offset // parent_rows
    assert largest_q < 16 and tiles >= 2 * 16
    center = 8
    planes = 3 * levels
    half = tiles // 2

    row_offset = nest_offsets[0, 0]
    col_offset = nest_offsets[0, 1]
    q = row_offset // parent_rows
    r = row_offset - q * parent_rows

    nest_fields = nest_state[:, :, 0]
    above3 = shift_from(nest_fields[:, :, nest_rows - 3 :], "tile", -1, tiles)
    below3 = shift_from(nest_fields[:, :, :3], "tile", 1, tiles)

    sound_factor = 1.0 - terrain.astype(jnp.float32) / terrain_scale
    halo_fields = parent_state[0:3:2]
    padded = extended_2(halo_fields, ((("grp", "tile"), 2),), 1)
    zonal_ext = jnp.pad(parent_state[1], ((0, 0), (1, 1), (0, 0)))
    extended = jnp.stack([padded[0], zonal_ext, padded[1]])
    factor_ext = jnp.pad(sound_factor, ((1, 1), (0, 0)))
    edge_zeros = jnp.zeros((levels, parent_rows + 2), jnp.float32)
    advanced = substep(extended, factor_ext, parent_courant, edge_zeros, edge_zeros)[:, :, 1:-1]

    window = lax.dynamic_slice_in_dim(advanced, col_offset - 1, coarse_cols + 2, axis=3)
    factor_window = lax.dynamic_slice_in_dim(sound_factor, col_offset, coarse_cols, axis=1)
    east_col = window[0, :, :, -1].T
    west_col = window[1, :, :, 0].T
    edge_plane = jnp.concatenate(
        [east_col, west_col, jnp.zeros((parent_rows, coarse_cols - 2 * levels), jnp.float32)], axis=1
    )
    rows_here = jnp.concatenate(
        [
            window[..., 1:-1].reshape(planes, parent_rows, coarse_cols),
            factor_window[None],
            edge_plane[None],
        ],
        axis=0,
    )
    above3, below3, rows_here = lax.optimization_barrier((above3, below3, rows_here))
    last_before = shift_from(rows_here[:, parent_rows - 1], "tile", -1, tiles)
    rows_after = shift_from(rows_here, "tile", 1, tiles)
    joined = jnp.concatenate([last_before[:, None], rows_here, rows_after], axis=1)
    block = lax.dynamic_slice_in_dim(joined, r, parent_rows, axis=1)
    low = q & 3
    bit2 = ((q >> 2) & 1) == 1
    bit3 = ((q >> 3) & 1) == 1
    block = pick(block, [(-center, jnp.logical_not(bit3))], tiles)
    block = pick(block, [(1, low == 1), (2, low == 2), (3, low == 3)], tiles)
    block = pick(block, [(4, bit2)], tiles)
    to_even = lax.ppermute(block, "tile", [(m + center, 2 * m) for m in range(half)])
    to_odd = lax.ppermute(block, "tile", [(m + center, 2 * m + 1) for m in range(half)])
    next_rows = jnp.transpose(block[:, : foot_rows - coarse_rows], (1, 0, 2))
    next_odd = lax.ppermute(next_rows, "tile", [(m + center + 1, 2 * m + 1) for m in range(half)])
    odd_rows = jnp.concatenate([to_odd[:, coarse_rows:], jnp.transpose(next_odd, (1, 0, 2))], axis=1)
    footprint = jnp.where(tile_index % 2 == 0, to_even[:, :foot_rows], odd_rows)

    widen = repeat_matrix(coarse_cols, 3)
    heighten = repeat_matrix(foot_rows, 3).T
    inner = jnp.einsum("pic,cj->pij", footprint[: planes + 1], widen, precision=HIGHEST)
    expanded = jnp.einsum("ri,pij->prj", heighten, inner, precision=HIGHEST)
    injected = expanded[:planes].reshape(3, levels, 3 * foot_rows, nest_cols)
    nest_factor = expanded[planes]
    east_rows = jnp.repeat(footprint[planes + 1, :, 0:levels].T, 3, axis=1)
    west_rows = jnp.repeat(footprint[planes + 1, :, levels : 2 * levels].T, 3, axis=1)

    local_rows = jnp.arange(3 * foot_rows, dtype=jnp.int32) - 3
    global_rows = nest_rows * tile_index + local_rows
    outside = ((global_rows < 0) | (global_rows >= nest_total))[None, None, :, None]
    fields = jnp.concatenate([above3, nest_fields, below3], axis=2)
    for _ in range(SUBSTEPS):
        fields = jnp.where(outside, injected, fields)
        stepped = substep(fields, nest_factor, nest_courant, east_rows, west_rows)
        fields = stepped + nudge_rate * (injected - stepped)
    new_nest = fields[:, :, 3 : 3 + nest_rows]

    narrow = repeat_matrix(coarse_cols, 3).T
    shorten = repeat_matrix(coarse_rows, 3)
    col_sums = jnp.einsum("plrj,jc->plrc", new_nest, narrow, precision=HIGHEST)
    sums = jnp.einsum("kr,plrc->kplc", shorten, col_sums, precision=HIGHEST)
    means = (sums / 9.0).reshape(coarse_rows, planes, coarse_cols)

    gathered = [
        lax.ppermute(
            means, "tile", [(2 * m + k, m + center) for m in range(half + 1) if 0 <= 2 * m + k < tiles]
        )
        for k in (-2, -1, 0, 1)
    ]
    both = jnp.concatenate(gathered, axis=0)
    back = lax.dynamic_slice_in_dim(both, parent_rows - r, parent_rows, axis=0)
    back = pick(back, [(center, jnp.logical_not(bit3))], tiles)
    back = pick(back, [(-1, low == 1), (-2, low == 2), (-3, low == 3)], tiles)
    back = pick(back, [(-4, bit2)], tiles)
    placed = jnp.transpose(back, (1, 0, 2)).reshape(3, levels, parent_rows, coarse_cols)
    band_row = parent_rows * tile_index + jnp.arange(parent_rows, dtype=jnp.int32) - row_offset
    covered = ((band_row >= 0) & (band_row < coarse_total))[None, None, :, None]
    previous = lax.dynamic_slice_in_dim(advanced, col_offset, coarse_cols, axis=3)
    merged = jnp.where(covered, placed, previous)
    new_parent = lax.dynamic_update_slice_in_dim(advanced, merged, col_offset, axis=3)
    return (new_parent, new_nest[:, :, None])


def solution(mesh):
    placed = (
        P(None, None, ("grp", "tile"), None),
        P(("grp", "tile"), None),
        P(None, None, "grp", "tile", None),
        P("grp", None),
    )
    return jax.shard_map(
        local,
        mesh=mesh,
        in_specs=placed,
        out_specs=(P(None, None, ("grp", "tile"), None), P(None, None, "grp", "tile", None)),
        check_vma=False,
    )
```

```python
import jax
import jax.numpy as jnp
from jax import lax
from jax.sharding import PartitionSpec as P

SUBSTEPS = 3


parent_courant = 0.35
nest_courant = 0.35
nudge_rate = 0.2
terrain_scale = 6000.0

HIGHEST = lax.Precision.HIGHEST


def shift_from(value, axis, offset, devices):
    pairs = [(d + offset, d) for d in range(devices) if 0 <= d + offset < devices]
    return lax.ppermute(value, axis, pairs)


def extended_2(value, sides, width):
    for axis, dim in sides:
        devices, length = (lax.axis_size(axis), value.shape[dim])
        up = [(i, (i + 1) % devices) for i in range(devices - 1)]
        down = [(j, i) for i, j in up]
        last = lax.slice_in_dim(value, length - width, length, axis=dim)
        first = lax.slice_in_dim(value, 0, width, axis=dim)
        before = lax.ppermute(last, axis, up)
        after = lax.ppermute(first, axis, down)
        value = jnp.concatenate([before, value, after], axis=dim)
    return value


def substep(fields, sound_factor, courant, east_edge, west_edge):
    pressure = fields[0]
    zonal_wind = fields[1]
    merid_wind = fields[2]
    east_side = jnp.concatenate([pressure[..., 1:], east_edge[..., None]], axis=-1)
    zonal_next = zonal_wind - courant * (east_side - pressure)
    below_side = jnp.concatenate(
        [pressure[..., 1:, :], jnp.zeros_like(pressure[..., :1, :])], axis=-2
    )
    merid_next = merid_wind - courant * (below_side - pressure)
    west_side = jnp.concatenate([west_edge[..., None], zonal_next[..., :-1]], axis=-1)
    above_side = jnp.concatenate(
        [jnp.zeros_like(merid_next[..., :1, :]), merid_next[..., :-1, :]], axis=-2
    )
    pressure_next = pressure - courant * sound_factor * (
        zonal_next - west_side + (merid_next - above_side)
    )
    return jnp.stack([pressure_next, zonal_next, merid_next])


def repeat_matrix(small, factor):
    rows = jnp.arange(small, dtype=jnp.int32)[:, None]
    cols = jnp.arange(small * factor, dtype=jnp.int32)[None, :] // factor
    return (rows == cols).astype(jnp.float32)


def rotate(value, options, slab, tiles):
    out = value
    for offset, predicate in options:
        pairs = [(s + (w + offset) % slab, s + w) for s in range(0, tiles, slab) for w in range(slab)]
        out = jnp.where(predicate, lax.ppermute(value, "tile", pairs), out)
    return out


def pick(value, options, tiles):
    out = value
    for offset, predicate in options:
        out = jnp.where(predicate, shift_from(value, "tile", offset, tiles), out)
    return out


def local(parent_state, terrain, nest_state, nest_offsets):
    tiles = lax.axis_size("tile")
    tile_index = lax.axis_index("tile")
    levels = parent_state.shape[1]
    parent_rows = parent_state.shape[2]
    nest_rows = nest_state.shape[3]
    nest_cols = nest_state.shape[4]
    coarse_rows = nest_rows // 3
    coarse_cols = nest_cols // 3
    foot_rows = coarse_rows + 2
    assert parent_rows == 2 * coarse_rows and 2 * levels <= coarse_cols
    band_rows = parent_rows * tiles
    nest_total = nest_rows * tiles
    coarse_total = nest_total // 3
    largest_offset = band_rows - coarse_total - 1
    largest_q = largest_offset // parent_rows
    assert largest_q < 16 and tiles % 8 == 0 and tiles >= 32
    center = 8
    planes = 3 * levels
    half = tiles // 2

    row_offset = nest_offsets[0, 0]
    col_offset = nest_offsets[0, 1]
    q = row_offset // parent_rows
    r = row_offset - q * parent_rows

    nest_fields = nest_state[:, :, 0]
    above3 = shift_from(nest_fields[:, :, nest_rows - 3 :], "tile", -1, tiles)
    below3 = shift_from(nest_fields[:, :, :3], "tile", 1, tiles)

    sound_factor = 1.0 - terrain.astype(jnp.float32) / terrain_scale
    halo_fields = parent_state[0:3:2]
    padded = extended_2(halo_fields, ((("grp", "tile"), 2),), 1)
    zonal_ext = jnp.pad(parent_state[1], ((0, 0), (1, 1), (0, 0)))
    extended = jnp.stack([padded[0], zonal_ext, padded[1]])
    factor_ext = jnp.pad(sound_factor, ((1, 1), (0, 0)))
    edge_zeros = jnp.zeros((levels, parent_rows + 2), jnp.float32)
    advanced = substep(extended, factor_ext, parent_courant, edge_zeros, edge_zeros)[:, :, 1:-1]

    window = lax.dynamic_slice_in_dim(advanced, col_offset - 1, coarse_cols + 2, axis=3)
    factor_window = lax.dynamic_slice_in_dim(sound_factor, col_offset, coarse_cols, axis=1)
    east_col = window[0, :, :, -1].T
    west_col = window[1, :, :, 0].T
    edge_plane = jnp.concatenate(
        [east_col, west_col, jnp.zeros((parent_rows, coarse_cols - 2 * levels), jnp.float32)], axis=1
    )
    rows_here = jnp.concatenate(
        [
            window[..., 1:-1].reshape(planes, parent_rows, coarse_cols),
            factor_window[None],
            edge_plane[None],
        ],
        axis=0,
    )
    above3, below3, rows_here = lax.optimization_barrier((above3, below3, rows_here))
    last_before = shift_from(rows_here[:, parent_rows - 1], "tile", -1, tiles)
    rows_after = shift_from(rows_here, "tile", 1, tiles)
    joined = jnp.concatenate([last_before[:, None], rows_here, rows_after], axis=1)
    block = lax.dynamic_slice_in_dim(joined, r, parent_rows, axis=1)
    low = q & 3
    bit2 = ((q >> 2) & 1) == 1
    bit3 = ((q >> 3) & 1) == 1
    low3 = q & (center - 1)
    slab_pos = tile_index % center
    block = rotate(block, [(1, low == 1), (2, low == 2), (3, low == 3)], center, tiles)
    block = rotate(block, [(4, bit2)], center, tiles)
    carry = (slab_pos + low3 >= center).astype(jnp.int32)
    slab_shift = bit3.astype(jnp.int32) + carry - 1
    block = pick(block, [(-center, slab_shift == -1), (center, slab_shift == 1)], tiles)
    to_even = lax.ppermute(block, "tile", [(m + center, 2 * m) for m in range(half)])
    to_odd = lax.ppermute(block, "tile", [(m + center, 2 * m + 1) for m in range(half)])
    next_rows = jnp.transpose(block[:, : foot_rows - coarse_rows], (1, 0, 2))
    next_odd = lax.ppermute(next_rows, "tile", [(m + center + 1, 2 * m + 1) for m in range(half)])
    odd_rows = jnp.concatenate([to_odd[:, coarse_rows:], jnp.transpose(next_odd, (1, 0, 2))], axis=1)
    footprint = jnp.where(tile_index % 2 == 0, to_even[:, :foot_rows], odd_rows)

    widen = repeat_matrix(coarse_cols, 3)
    heighten = repeat_matrix(foot_rows, 3).T
    inner = jnp.einsum("pic,cj->pij", footprint[: planes + 1], widen, precision=HIGHEST)
    expanded = jnp.einsum("ri,pij->prj", heighten, inner, precision=HIGHEST)
    injected = expanded[:planes].reshape(3, levels, 3 * foot_rows, nest_cols)
    nest_factor = expanded[planes]
    east_rows = jnp.repeat(footprint[planes + 1, :, 0:levels].T, 3, axis=1)
    west_rows = jnp.repeat(footprint[planes + 1, :, levels : 2 * levels].T, 3, axis=1)

    local_rows = jnp.arange(3 * foot_rows, dtype=jnp.int32) - 3
    global_rows = nest_rows * tile_index + local_rows
    outside = ((global_rows < 0) | (global_rows >= nest_total))[None, None, :, None]
    fields = jnp.concatenate([above3, nest_fields, below3], axis=2)
    for _ in range(SUBSTEPS):
        fields = jnp.where(outside, injected, fields)
        stepped = substep(fields, nest_factor, nest_courant, east_rows, west_rows)
        fields = stepped + nudge_rate * (injected - stepped)
    new_nest = fields[:, :, 3 : 3 + nest_rows]

    narrow = repeat_matrix(coarse_cols, 3).T
    shorten = repeat_matrix(coarse_rows, 3)
    col_sums = jnp.einsum("plrj,jc->plrc", new_nest, narrow, precision=HIGHEST)
    sums = jnp.einsum("kr,plrc->kplc", shorten, col_sums, precision=HIGHEST)
    means = (sums / 9.0).reshape(coarse_rows, planes, coarse_cols)

    gathered = [
        lax.ppermute(
            means, "tile", [(2 * m + k, m + center) for m in range(half + 1) if 0 <= 2 * m + k < tiles]
        )
        for k in (-2, -1, 0, 1)
    ]
    both = jnp.concatenate(gathered, axis=0)
    back = lax.dynamic_slice_in_dim(both, parent_rows - r, parent_rows, axis=0)
    back = pick(back, [(center, jnp.logical_not(bit3))], tiles)
    back = pick(back, [(-1, low == 1), (-2, low == 2), (-3, low == 3)], tiles)
    back = pick(back, [(-4, bit2)], tiles)
    placed = jnp.transpose(back, (1, 0, 2)).reshape(3, levels, parent_rows, coarse_cols)
    band_row = parent_rows * tile_index + jnp.arange(parent_rows, dtype=jnp.int32) - row_offset
    covered = ((band_row >= 0) & (band_row < coarse_total))[None, None, :, None]
    previous = lax.dynamic_slice_in_dim(advanced, col_offset, coarse_cols, axis=3)
    merged = jnp.where(covered, placed, previous)
    new_parent = lax.dynamic_update_slice_in_dim(advanced, merged, col_offset, axis=3)
    return (new_parent, new_nest[:, :, None])


def solution(mesh):
    placed = (
        P(None, None, ("grp", "tile"), None),
        P(("grp", "tile"), None),
        P(None, None, "grp", "tile", None),
        P("grp", None),
    )
    return jax.shard_map(
        local,
        mesh=mesh,
        in_specs=placed,
        out_specs=(P(None, None, ("grp", "tile"), None), P(None, None, "grp", "tile", None)),
        check_vma=False,
    )
```

```python
import jax
import jax.numpy as jnp
from jax import lax
from jax.sharding import PartitionSpec as P

SUBSTEPS = 3


parent_courant = 0.35
nest_courant = 0.35
nudge_rate = 0.2
terrain_scale = 6000.0

HIGHEST = lax.Precision.HIGHEST


def shift_from(value, axis, offset, devices):
    pairs = [(d + offset, d) for d in range(devices) if 0 <= d + offset < devices]
    return lax.ppermute(value, axis, pairs)


def extended_2(value, sides, width):
    for axis, dim in sides:
        devices, length = (lax.axis_size(axis), value.shape[dim])
        up = [(i, (i + 1) % devices) for i in range(devices - 1)]
        down = [(j, i) for i, j in up]
        last = lax.slice_in_dim(value, length - width, length, axis=dim)
        first = lax.slice_in_dim(value, 0, width, axis=dim)
        before = lax.ppermute(last, axis, up)
        after = lax.ppermute(first, axis, down)
        value = jnp.concatenate([before, value, after], axis=dim)
    return value


def substep(fields, sound_factor, courant, east_edge, west_edge):
    pressure = fields[0]
    zonal_wind = fields[1]
    merid_wind = fields[2]
    east_side = jnp.concatenate([pressure[..., 1:], east_edge[..., None]], axis=-1)
    zonal_next = zonal_wind - courant * (east_side - pressure)
    below_side = jnp.concatenate(
        [pressure[..., 1:, :], jnp.zeros_like(pressure[..., :1, :])], axis=-2
    )
    merid_next = merid_wind - courant * (below_side - pressure)
    west_side = jnp.concatenate([west_edge[..., None], zonal_next[..., :-1]], axis=-1)
    above_side = jnp.concatenate(
        [jnp.zeros_like(merid_next[..., :1, :]), merid_next[..., :-1, :]], axis=-2
    )
    pressure_next = pressure - courant * sound_factor * (
        zonal_next - west_side + (merid_next - above_side)
    )
    return jnp.stack([pressure_next, zonal_next, merid_next])


def repeat_matrix(small, factor):
    rows = jnp.arange(small, dtype=jnp.int32)[:, None]
    cols = jnp.arange(small * factor, dtype=jnp.int32)[None, :] // factor
    return (rows == cols).astype(jnp.float32)


def rotate(value, options, slab, tiles):
    out = value
    for offset, predicate in options:
        pairs = [(s + (w + offset) % slab, s + w) for s in range(0, tiles, slab) for w in range(slab)]
        out = jnp.where(predicate, lax.ppermute(value, "tile", pairs), out)
    return out


def pick(value, options, tiles):
    out = value
    for offset, predicate in options:
        out = jnp.where(predicate, shift_from(value, "tile", offset, tiles), out)
    return out


def local(parent_state, terrain, nest_state, nest_offsets):
    tiles = lax.axis_size("tile")
    tile_index = lax.axis_index("tile")
    levels = parent_state.shape[1]
    parent_rows = parent_state.shape[2]
    nest_rows = nest_state.shape[3]
    nest_cols = nest_state.shape[4]
    coarse_rows = nest_rows // 3
    coarse_cols = nest_cols // 3
    foot_rows = coarse_rows + 2
    assert parent_rows == 2 * coarse_rows and 2 * levels <= coarse_cols
    band_rows = parent_rows * tiles
    nest_total = nest_rows * tiles
    coarse_total = nest_total // 3
    largest_offset = band_rows - coarse_total - 1
    largest_q = largest_offset // parent_rows
    assert largest_q < 16 and tiles % 8 == 0 and tiles >= 32
    center = 8
    planes = 3 * levels
    half = tiles // 2

    row_offset = nest_offsets[0, 0]
    col_offset = nest_offsets[0, 1]
    q = row_offset // parent_rows
    r = row_offset - q * parent_rows

    nest_fields = nest_state[:, :, 0]
    above3 = shift_from(nest_fields[:, :, nest_rows - 3 :], "tile", -1, tiles)
    below3 = shift_from(nest_fields[:, :, :3], "tile", 1, tiles)

    sound_factor = 1.0 - terrain.astype(jnp.float32) / terrain_scale
    halo_fields = parent_state[0:3:2]
    padded = extended_2(halo_fields, ((("grp", "tile"), 2),), 1)
    zonal_ext = jnp.pad(parent_state[1], ((0, 0), (1, 1), (0, 0)))
    extended = jnp.stack([padded[0], zonal_ext, padded[1]])
    factor_ext = jnp.pad(sound_factor, ((1, 1), (0, 0)))
    edge_zeros = jnp.zeros((levels, parent_rows + 2), jnp.float32)
    advanced = substep(extended, factor_ext, parent_courant, edge_zeros, edge_zeros)[:, :, 1:-1]

    window = lax.dynamic_slice_in_dim(advanced, col_offset - 1, coarse_cols + 2, axis=3)
    factor_window = lax.dynamic_slice_in_dim(sound_factor, col_offset, coarse_cols, axis=1)
    east_col = window[0, :, :, -1].T
    west_col = window[1, :, :, 0].T
    edge_plane = jnp.concatenate(
        [east_col, west_col, jnp.zeros((parent_rows, coarse_cols - 2 * levels), jnp.float32)], axis=1
    )
    rows_here = jnp.concatenate(
        [
            window[..., 1:-1].reshape(planes, parent_rows, coarse_cols),
            factor_window[None],
            edge_plane[None],
        ],
        axis=0,
    )
    above3, below3, block = lax.optimization_barrier((above3, below3, rows_here))
    low = q & 3
    bit2 = ((q >> 2) & 1) == 1
    bit3 = ((q >> 3) & 1) == 1
    low3 = q & (center - 1)
    slab_pos = tile_index % center
    block = rotate(block, [(1, low == 1), (2, low == 2), (3, low == 3)], center, tiles)
    block = rotate(block, [(4, bit2)], center, tiles)
    carry = (slab_pos + low3 >= center).astype(jnp.int32)
    slab_shift = bit3.astype(jnp.int32) + carry - 1
    block = pick(block, [(-center, slab_shift == -1), (center, slab_shift == 1)], tiles)
    extra = foot_rows - 2
    own_even = lax.ppermute(block, "tile", [(m + center, 2 * m) for m in range(half)])
    last_even = lax.ppermute(
        block[:, parent_rows - 1], "tile", [(m + center - 1, 2 * m) for m in range(half)]
    )
    first_rows = jnp.transpose(block[:, :extra], (1, 0, 2))
    next_even = lax.ppermute(first_rows, "tile", [(m + center + 1, 2 * m) for m in range(half)])
    own_odd = lax.ppermute(block, "tile", [(m + center, 2 * m + 1) for m in range(half)])
    next_odd = lax.ppermute(block, "tile", [(m + center + 1, 2 * m + 1) for m in range(half)])
    even_rows = jnp.concatenate(
        [last_even[:, None], own_even, jnp.transpose(next_even, (1, 0, 2))], axis=1
    )
    odd_rows = jnp.concatenate([own_odd, next_odd], axis=1)
    footprint = jnp.where(
        tile_index % 2 == 0,
        lax.dynamic_slice_in_dim(even_rows, r, foot_rows, axis=1),
        lax.dynamic_slice_in_dim(odd_rows, r + coarse_rows - 1, foot_rows, axis=1),
    )

    widen = repeat_matrix(coarse_cols, 3)
    heighten = repeat_matrix(foot_rows, 3).T
    inner = jnp.einsum("pic,cj->pij", footprint[: planes + 1], widen, precision=HIGHEST)
    expanded = jnp.einsum("ri,pij->prj", heighten, inner, precision=HIGHEST)
    injected = expanded[:planes].reshape(3, levels, 3 * foot_rows, nest_cols)
    nest_factor = expanded[planes]
    east_rows = jnp.repeat(footprint[planes + 1, :, 0:levels].T, 3, axis=1)
    west_rows = jnp.repeat(footprint[planes + 1, :, levels : 2 * levels].T, 3, axis=1)

    local_rows = jnp.arange(3 * foot_rows, dtype=jnp.int32) - 3
    global_rows = nest_rows * tile_index + local_rows
    outside = ((global_rows < 0) | (global_rows >= nest_total))[None, None, :, None]
    fields = jnp.concatenate([above3, nest_fields, below3], axis=2)
    for _ in range(SUBSTEPS):
        fields = jnp.where(outside, injected, fields)
        stepped = substep(fields, nest_factor, nest_courant, east_rows, west_rows)
        fields = stepped + nudge_rate * (injected - stepped)
    new_nest = fields[:, :, 3 : 3 + nest_rows]

    narrow = repeat_matrix(coarse_cols, 3).T
    shorten = repeat_matrix(coarse_rows, 3)
    col_sums = jnp.einsum("plrj,jc->plrc", new_nest, narrow, precision=HIGHEST)
    sums = jnp.einsum("kr,plrc->kplc", shorten, col_sums, precision=HIGHEST)
    means = (sums / 9.0).reshape(coarse_rows, planes, coarse_cols)

    gathered = [
        lax.ppermute(
            means, "tile", [(2 * m + k, m + center) for m in range(half + 1) if 0 <= 2 * m + k < tiles]
        )
        for k in (-2, -1, 0, 1)
    ]
    both = jnp.concatenate(gathered, axis=0)
    back = lax.dynamic_slice_in_dim(both, parent_rows - r, parent_rows, axis=0)
    back = pick(back, [(center, jnp.logical_not(bit3))], tiles)
    back = pick(back, [(-1, low == 1), (-2, low == 2), (-3, low == 3)], tiles)
    back = pick(back, [(-4, bit2)], tiles)
    placed = jnp.transpose(back, (1, 0, 2)).reshape(3, levels, parent_rows, coarse_cols)
    band_row = parent_rows * tile_index + jnp.arange(parent_rows, dtype=jnp.int32) - row_offset
    covered = ((band_row >= 0) & (band_row < coarse_total))[None, None, :, None]
    previous = lax.dynamic_slice_in_dim(advanced, col_offset, coarse_cols, axis=3)
    merged = jnp.where(covered, placed, previous)
    new_parent = lax.dynamic_update_slice_in_dim(advanced, merged, col_offset, axis=3)
    return (new_parent, new_nest[:, :, None])


def solution(mesh):
    placed = (
        P(None, None, ("grp", "tile"), None),
        P(("grp", "tile"), None),
        P(None, None, "grp", "tile", None),
        P("grp", None),
    )
    return jax.shard_map(
        local,
        mesh=mesh,
        in_specs=placed,
        out_specs=(P(None, None, ("grp", "tile"), None), P(None, None, "grp", "tile", None)),
        check_vma=False,
    )
```

```python
import jax
import jax.numpy as jnp
from jax import lax
from jax.sharding import PartitionSpec as P

SUBSTEPS = 3


parent_courant = 0.35
nest_courant = 0.35
nudge_rate = 0.2
terrain_scale = 6000.0

HIGHEST = lax.Precision.HIGHEST


def shift_from(value, axis, offset, devices):
    pairs = [(d + offset, d) for d in range(devices) if 0 <= d + offset < devices]
    return lax.ppermute(value, axis, pairs)


def extended_2(value, sides, width):
    for axis, dim in sides:
        devices, length = (lax.axis_size(axis), value.shape[dim])
        up = [(i, (i + 1) % devices) for i in range(devices - 1)]
        down = [(j, i) for i, j in up]
        last = lax.slice_in_dim(value, length - width, length, axis=dim)
        first = lax.slice_in_dim(value, 0, width, axis=dim)
        before = lax.ppermute(last, axis, up)
        after = lax.ppermute(first, axis, down)
        value = jnp.concatenate([before, value, after], axis=dim)
    return value


def substep(fields, sound_factor, courant, east_edge, west_edge):
    pressure = fields[0]
    zonal_wind = fields[1]
    merid_wind = fields[2]
    east_side = jnp.concatenate([pressure[..., 1:], east_edge[..., None]], axis=-1)
    zonal_next = zonal_wind - courant * (east_side - pressure)
    below_side = jnp.concatenate(
        [pressure[..., 1:, :], jnp.zeros_like(pressure[..., :1, :])], axis=-2
    )
    merid_next = merid_wind - courant * (below_side - pressure)
    west_side = jnp.concatenate([west_edge[..., None], zonal_next[..., :-1]], axis=-1)
    above_side = jnp.concatenate(
        [jnp.zeros_like(merid_next[..., :1, :]), merid_next[..., :-1, :]], axis=-2
    )
    pressure_next = pressure - courant * sound_factor * (
        zonal_next - west_side + (merid_next - above_side)
    )
    return jnp.stack([pressure_next, zonal_next, merid_next])


def repeat_matrix(small, factor):
    rows = jnp.arange(small, dtype=jnp.int32)[:, None]
    cols = jnp.arange(small * factor, dtype=jnp.int32)[None, :] // factor
    return (rows == cols).astype(jnp.float32)


def rotate(value, options, slab, tiles):
    out = value
    for offset, predicate in options:
        pairs = [(s + (w + offset) % slab, s + w) for s in range(0, tiles, slab) for w in range(slab)]
        out = jnp.where(predicate, lax.ppermute(value, "tile", pairs), out)
    return out


def pick(value, options, tiles):
    out = value
    for offset, predicate in options:
        out = jnp.where(predicate, shift_from(value, "tile", offset, tiles), out)
    return out


def local(parent_state, terrain, nest_state, nest_offsets):
    tiles = lax.axis_size("tile")
    tile_index = lax.axis_index("tile")
    levels = parent_state.shape[1]
    parent_rows = parent_state.shape[2]
    nest_rows = nest_state.shape[3]
    nest_cols = nest_state.shape[4]
    coarse_rows = nest_rows // 3
    coarse_cols = nest_cols // 3
    foot_rows = coarse_rows + 2
    assert parent_rows == 2 * coarse_rows and 2 * levels <= coarse_cols
    band_rows = parent_rows * tiles
    nest_total = nest_rows * tiles
    coarse_total = nest_total // 3
    largest_offset = band_rows - coarse_total - 1
    largest_q = largest_offset // parent_rows
    assert largest_q < 16 and tiles % 8 == 0 and tiles >= 32
    center = 8
    planes = 3 * levels
    half = tiles // 2

    row_offset = nest_offsets[0, 0]
    col_offset = nest_offsets[0, 1]
    q = row_offset // parent_rows
    r = row_offset - q * parent_rows

    nest_fields = nest_state[:, :, 0]
    above3 = shift_from(jnp.moveaxis(nest_fields[:, :, nest_rows - 3 :], 2, 0), "tile", -1, tiles)
    below3 = shift_from(jnp.moveaxis(nest_fields[:, :, :3], 2, 0), "tile", 1, tiles)

    sound_factor = 1.0 - terrain.astype(jnp.float32) / terrain_scale
    halo_fields = parent_state[0:3:2]
    line = ("grp", "tile")
    lines = lax.axis_size(line)
    row_above = shift_from(halo_fields[:, :, parent_rows - 1], line, -1, lines)
    row_below = shift_from(halo_fields[:, :, 0], line, 1, lines)
    padded = jnp.concatenate([row_above[:, :, None], halo_fields, row_below[:, :, None]], axis=2)
    zonal_ext = jnp.pad(parent_state[1], ((0, 0), (1, 1), (0, 0)))
    extended = jnp.stack([padded[0], zonal_ext, padded[1]])
    factor_ext = jnp.pad(sound_factor, ((1, 1), (0, 0)))
    edge_zeros = jnp.zeros((levels, parent_rows + 2), jnp.float32)
    advanced = substep(extended, factor_ext, parent_courant, edge_zeros, edge_zeros)[:, :, 1:-1]

    window = lax.dynamic_slice_in_dim(advanced, col_offset - 1, coarse_cols + 2, axis=3)
    factor_window = lax.dynamic_slice_in_dim(sound_factor, col_offset, coarse_cols, axis=1)
    east_col = window[0, :, :, -1].T
    west_col = window[1, :, :, 0].T
    edge_plane = jnp.concatenate(
        [east_col, west_col, jnp.zeros((parent_rows, coarse_cols - 2 * levels), jnp.float32)], axis=1
    )
    rows_here = jnp.concatenate(
        [
            window[..., 1:-1].reshape(planes, parent_rows, coarse_cols),
            factor_window[None],
            edge_plane[None],
        ],
        axis=0,
    )
    above3, below3, block = lax.optimization_barrier((above3, below3, rows_here))
    low = q & 3
    bit2 = ((q >> 2) & 1) == 1
    bit3 = ((q >> 3) & 1) == 1
    low3 = q & (center - 1)
    slab_pos = tile_index % center
    block = rotate(block, [(1, low == 1), (2, low == 2), (3, low == 3)], center, tiles)
    block = rotate(block, [(4, bit2)], center, tiles)
    carry = (slab_pos + low3 >= center).astype(jnp.int32)
    slab_shift = bit3.astype(jnp.int32) + carry - 1
    block = pick(block, [(-center, slab_shift == -1), (center, slab_shift == 1)], tiles)
    extra = foot_rows - 2
    own_even = lax.ppermute(block, "tile", [(m + center, 2 * m) for m in range(half)])
    last_even = lax.ppermute(
        block[:, parent_rows - 1], "tile", [(m + center - 1, 2 * m) for m in range(half)]
    )
    first_rows = jnp.transpose(block[:, :extra], (1, 0, 2))
    next_even = lax.ppermute(first_rows, "tile", [(m + center + 1, 2 * m) for m in range(half)])
    own_odd = lax.ppermute(block, "tile", [(m + center, 2 * m + 1) for m in range(half)])
    next_odd = lax.ppermute(block, "tile", [(m + center + 1, 2 * m + 1) for m in range(half)])
    even_rows = jnp.concatenate(
        [last_even[:, None], own_even, jnp.transpose(next_even, (1, 0, 2))], axis=1
    )
    odd_rows = jnp.concatenate([own_odd, next_odd], axis=1)
    footprint = jnp.where(
        tile_index % 2 == 0,
        lax.dynamic_slice_in_dim(even_rows, r, foot_rows, axis=1),
        lax.dynamic_slice_in_dim(odd_rows, r + coarse_rows - 1, foot_rows, axis=1),
    )

    widen = repeat_matrix(coarse_cols, 3)
    heighten = repeat_matrix(foot_rows, 3).T
    inner = jnp.einsum("pic,cj->pij", footprint[: planes + 1], widen, precision=HIGHEST)
    expanded = jnp.einsum("ri,pij->prj", heighten, inner, precision=HIGHEST)
    injected = expanded[:planes].reshape(3, levels, 3 * foot_rows, nest_cols)
    nest_factor = expanded[planes]
    east_rows = jnp.repeat(footprint[planes + 1, :, 0:levels].T, 3, axis=1)
    west_rows = jnp.repeat(footprint[planes + 1, :, levels : 2 * levels].T, 3, axis=1)

    local_rows = jnp.arange(3 * foot_rows, dtype=jnp.int32) - 3
    global_rows = nest_rows * tile_index + local_rows
    outside = ((global_rows < 0) | (global_rows >= nest_total))[None, None, :, None]
    fields = jnp.concatenate(
        [jnp.moveaxis(above3, 0, 2), nest_fields, jnp.moveaxis(below3, 0, 2)], axis=2
    )
    for _ in range(SUBSTEPS):
        fields = jnp.where(outside, injected, fields)
        stepped = substep(fields, nest_factor, nest_courant, east_rows, west_rows)
        fields = stepped + nudge_rate * (injected - stepped)
    new_nest = fields[:, :, 3 : 3 + nest_rows]

    narrow = repeat_matrix(coarse_cols, 3).T
    shorten = repeat_matrix(coarse_rows, 3)
    col_sums = jnp.einsum("plrj,jc->plrc", new_nest, narrow, precision=HIGHEST)
    sums = jnp.einsum("kr,plrc->kplc", shorten, col_sums, precision=HIGHEST)
    means = (sums / 9.0).reshape(coarse_rows, planes, coarse_cols)

    gathered = [
        lax.ppermute(
            means, "tile", [(2 * m + k, m + center) for m in range(half + 1) if 0 <= 2 * m + k < tiles]
        )
        for k in (-2, -1, 0, 1)
    ]
    both = jnp.concatenate(gathered, axis=0)
    back = lax.dynamic_slice_in_dim(both, parent_rows - r, parent_rows, axis=0)
    back_carry = carry
    back_shift = bit3.astype(jnp.int32) + back_carry - 1
    back = pick(back, [(-center, back_shift == 1), (center, back_shift == -1)], tiles)
    back = rotate(back, [(-1, low == 1), (-2, low == 2), (-3, low == 3)], center, tiles)
    back = rotate(back, [(-4, bit2)], center, tiles)
    placed = jnp.transpose(back, (1, 0, 2)).reshape(3, levels, parent_rows, coarse_cols)
    band_row = parent_rows * tile_index + jnp.arange(parent_rows, dtype=jnp.int32) - row_offset
    covered = ((band_row >= 0) & (band_row < coarse_total))[None, None, :, None]
    previous = lax.dynamic_slice_in_dim(advanced, col_offset, coarse_cols, axis=3)
    merged = jnp.where(covered, placed, previous)
    new_parent = lax.dynamic_update_slice_in_dim(advanced, merged, col_offset, axis=3)
    return (new_parent, new_nest[:, :, None])


def solution(mesh):
    placed = (
        P(None, None, ("grp", "tile"), None),
        P(("grp", "tile"), None),
        P(None, None, "grp", "tile", None),
        P("grp", None),
    )
    return jax.shard_map(
        local,
        mesh=mesh,
        in_specs=placed,
        out_specs=(P(None, None, ("grp", "tile"), None), P(None, None, "grp", "tile", None)),
        check_vma=False,
    )
```

```python
import jax
import jax.numpy as jnp
from jax import lax
from jax.sharding import PartitionSpec as P

SUBSTEPS = 3


parent_courant = 0.35
nest_courant = 0.35
nudge_rate = 0.2
terrain_scale = 6000.0

HIGHEST = lax.Precision.HIGHEST


def shift_from(value, axis, offset, devices):
    pairs = [(d + offset, d) for d in range(devices) if 0 <= d + offset < devices]
    return lax.ppermute(value, axis, pairs)


def extended_2(value, sides, width):
    for axis, dim in sides:
        devices, length = (lax.axis_size(axis), value.shape[dim])
        up = [(i, (i + 1) % devices) for i in range(devices - 1)]
        down = [(j, i) for i, j in up]
        last = lax.slice_in_dim(value, length - width, length, axis=dim)
        first = lax.slice_in_dim(value, 0, width, axis=dim)
        before = lax.ppermute(last, axis, up)
        after = lax.ppermute(first, axis, down)
        value = jnp.concatenate([before, value, after], axis=dim)
    return value


def substep(fields, sound_factor, courant, east_edge, west_edge):
    pressure = fields[0]
    zonal_wind = fields[1]
    merid_wind = fields[2]
    east_side = jnp.concatenate([pressure[..., 1:], east_edge[..., None]], axis=-1)
    zonal_next = zonal_wind - courant * (east_side - pressure)
    below_side = jnp.concatenate(
        [pressure[..., 1:, :], jnp.zeros_like(pressure[..., :1, :])], axis=-2
    )
    merid_next = merid_wind - courant * (below_side - pressure)
    west_side = jnp.concatenate([west_edge[..., None], zonal_next[..., :-1]], axis=-1)
    above_side = jnp.concatenate(
        [jnp.zeros_like(merid_next[..., :1, :]), merid_next[..., :-1, :]], axis=-2
    )
    pressure_next = pressure - courant * sound_factor * (
        zonal_next - west_side + (merid_next - above_side)
    )
    return jnp.stack([pressure_next, zonal_next, merid_next])


def repeat_matrix(small, factor):
    rows = jnp.arange(small, dtype=jnp.int32)[:, None]
    cols = jnp.arange(small * factor, dtype=jnp.int32)[None, :] // factor
    return (rows == cols).astype(jnp.float32)


def rotate(value, options, slab, tiles):
    out = value
    for offset, predicate in options:
        pairs = [(s + (w + offset) % slab, s + w) for s in range(0, tiles, slab) for w in range(slab)]
        out = jnp.where(predicate, lax.ppermute(value, "tile", pairs), out)
    return out


def pick(value, options, tiles):
    out = value
    for offset, predicate in options:
        out = jnp.where(predicate, shift_from(value, "tile", offset, tiles), out)
    return out


def local(parent_state, terrain, nest_state, nest_offsets):
    tiles = lax.axis_size("tile")
    tile_index = lax.axis_index("tile")
    levels = parent_state.shape[1]
    parent_rows = parent_state.shape[2]
    nest_rows = nest_state.shape[3]
    nest_cols = nest_state.shape[4]
    coarse_rows = nest_rows // 3
    coarse_cols = nest_cols // 3
    foot_rows = coarse_rows + 2
    assert parent_rows == 2 * coarse_rows and 2 * levels <= coarse_cols
    band_rows = parent_rows * tiles
    nest_total = nest_rows * tiles
    coarse_total = nest_total // 3
    largest_offset = band_rows - coarse_total - 1
    largest_q = largest_offset // parent_rows
    assert largest_q < 16 and tiles % 8 == 0 and tiles >= 32
    center = 8
    planes = 3 * levels
    half = tiles // 2

    row_offset = nest_offsets[0, 0]
    col_offset = nest_offsets[0, 1]
    q = row_offset // parent_rows
    r = row_offset - q * parent_rows

    nest_fields = nest_state[:, :, 0]
    above3 = shift_from(jnp.moveaxis(nest_fields[:, :, nest_rows - 3 :], 2, 0), "tile", -1, tiles)
    below3 = shift_from(jnp.moveaxis(nest_fields[:, :, :3], 2, 0), "tile", 1, tiles)

    sound_factor = 1.0 - terrain.astype(jnp.float32) / terrain_scale
    halo_fields = parent_state[0:3:2]
    line = ("grp", "tile")
    lines = lax.axis_size(line)
    row_above = shift_from(halo_fields[:, :, parent_rows - 1], line, -1, lines)
    row_below = shift_from(halo_fields[:, :, 0], line, 1, lines)
    padded = jnp.concatenate([row_above[:, :, None], halo_fields, row_below[:, :, None]], axis=2)
    zonal_ext = jnp.pad(parent_state[1], ((0, 0), (1, 1), (0, 0)))
    extended = jnp.stack([padded[0], zonal_ext, padded[1]])
    factor_ext = jnp.pad(sound_factor, ((1, 1), (0, 0)))
    edge_zeros = jnp.zeros((levels, parent_rows + 2), jnp.float32)
    advanced = substep(extended, factor_ext, parent_courant, edge_zeros, edge_zeros)[:, :, 1:-1]

    window = lax.dynamic_slice_in_dim(advanced, col_offset - 1, coarse_cols + 2, axis=3)
    factor_window = lax.dynamic_slice_in_dim(sound_factor, col_offset, coarse_cols, axis=1)
    east_col = window[0, :, :, -1].T
    west_col = window[1, :, :, 0].T
    edge_plane = jnp.concatenate(
        [east_col, west_col, jnp.zeros((parent_rows, coarse_cols - 2 * levels), jnp.float32)], axis=1
    )
    rows_here = jnp.concatenate(
        [
            window[..., 1:-1].reshape(planes, parent_rows, coarse_cols),
            factor_window[None],
            edge_plane[None],
        ],
        axis=0,
    )
    above3, below3, block = lax.optimization_barrier((above3, below3, rows_here))
    low = q & 3
    bit2 = ((q >> 2) & 1) == 1
    bit3 = ((q >> 3) & 1) == 1
    low3 = q & (center - 1)
    slab_pos = tile_index % center
    block = rotate(block, [(1, low == 1), (2, low == 2), (3, low == 3)], center, tiles)
    block = rotate(block, [(4, bit2)], center, tiles)
    carry = (slab_pos + low3 >= center).astype(jnp.int32)
    slab_shift = bit3.astype(jnp.int32) + carry - 1
    block = pick(block, [(-center, slab_shift == -1), (center, slab_shift == 1)], tiles)
    extra = foot_rows - 2
    own_even = lax.ppermute(block, "tile", [(m + center, 2 * m) for m in range(half)])
    last_even = lax.ppermute(
        block[:, parent_rows - 1], "tile", [(m + center - 1, 2 * m) for m in range(half)]
    )
    next_odd = lax.ppermute(block, "tile", [(m + center + 1, 2 * m + 1) for m in range(half)])
    own_odd = lax.ppermute(own_even, "tile", [(2 * m, 2 * m + 1) for m in range(half)])
    first_rows = jnp.transpose(next_odd[:, :extra], (1, 0, 2))
    next_even = lax.ppermute(first_rows, "tile", [(2 * m + 1, 2 * m) for m in range(half)])
    even_rows = jnp.concatenate(
        [last_even[:, None], own_even, jnp.transpose(next_even, (1, 0, 2))], axis=1
    )
    odd_rows = jnp.concatenate([own_odd, next_odd], axis=1)
    footprint = jnp.where(
        tile_index % 2 == 0,
        lax.dynamic_slice_in_dim(even_rows, r, foot_rows, axis=1),
        lax.dynamic_slice_in_dim(odd_rows, r + coarse_rows - 1, foot_rows, axis=1),
    )

    widen = repeat_matrix(coarse_cols, 3)
    heighten = repeat_matrix(foot_rows, 3).T
    inner = jnp.einsum("pic,cj->pij", footprint[: planes + 1], widen, precision=HIGHEST)
    expanded = jnp.einsum("ri,pij->prj", heighten, inner, precision=HIGHEST)
    injected = expanded[:planes].reshape(3, levels, 3 * foot_rows, nest_cols)
    nest_factor = expanded[planes]
    east_rows = jnp.repeat(footprint[planes + 1, :, 0:levels].T, 3, axis=1)
    west_rows = jnp.repeat(footprint[planes + 1, :, levels : 2 * levels].T, 3, axis=1)

    local_rows = jnp.arange(3 * foot_rows, dtype=jnp.int32) - 3
    global_rows = nest_rows * tile_index + local_rows
    outside = ((global_rows < 0) | (global_rows >= nest_total))[None, None, :, None]
    fields = jnp.concatenate(
        [jnp.moveaxis(above3, 0, 2), nest_fields, jnp.moveaxis(below3, 0, 2)], axis=2
    )
    for _ in range(SUBSTEPS):
        fields = jnp.where(outside, injected, fields)
        stepped = substep(fields, nest_factor, nest_courant, east_rows, west_rows)
        fields = stepped + nudge_rate * (injected - stepped)
    new_nest = fields[:, :, 3 : 3 + nest_rows]

    narrow = repeat_matrix(coarse_cols, 3).T
    shorten = repeat_matrix(coarse_rows, 3)
    col_sums = jnp.einsum("plrj,jc->plrc", new_nest, narrow, precision=HIGHEST)
    sums = jnp.einsum("kr,plrc->kplc", shorten, col_sums, precision=HIGHEST)
    means = (sums / 9.0).reshape(coarse_rows, planes, coarse_cols)

    gathered = [
        lax.ppermute(
            means, "tile", [(2 * m + k, m + center) for m in range(half + 1) if 0 <= 2 * m + k < tiles]
        )
        for k in (-2, -1, 0, 1)
    ]
    both = jnp.concatenate(gathered, axis=0)
    back = lax.dynamic_slice_in_dim(both, parent_rows - r, parent_rows, axis=0)
    back_carry = carry
    back_shift = bit3.astype(jnp.int32) + back_carry - 1
    back = pick(back, [(-center, back_shift == 1), (center, back_shift == -1)], tiles)
    back = rotate(back, [(-1, low == 1), (-2, low == 2), (-3, low == 3)], center, tiles)
    back = rotate(back, [(-4, bit2)], center, tiles)
    placed = jnp.transpose(back, (1, 0, 2)).reshape(3, levels, parent_rows, coarse_cols)
    band_row = parent_rows * tile_index + jnp.arange(parent_rows, dtype=jnp.int32) - row_offset
    covered = ((band_row >= 0) & (band_row < coarse_total))[None, None, :, None]
    previous = lax.dynamic_slice_in_dim(advanced, col_offset, coarse_cols, axis=3)
    merged = jnp.where(covered, placed, previous)
    new_parent = lax.dynamic_update_slice_in_dim(advanced, merged, col_offset, axis=3)
    return (new_parent, new_nest[:, :, None])


def solution(mesh):
    placed = (
        P(None, None, ("grp", "tile"), None),
        P(("grp", "tile"), None),
        P(None, None, "grp", "tile", None),
        P("grp", None),
    )
    return jax.shard_map(
        local,
        mesh=mesh,
        in_specs=placed,
        out_specs=(P(None, None, ("grp", "tile"), None), P(None, None, "grp", "tile", None)),
        check_vma=False,
    )
```

```python
import jax
import jax.numpy as jnp
from jax import lax
from jax.sharding import PartitionSpec as P

SUBSTEPS = 3


parent_courant = 0.35
nest_courant = 0.35
nudge_rate = 0.2
terrain_scale = 6000.0

HIGHEST = lax.Precision.HIGHEST


def shift_from(value, axis, offset, devices):
    pairs = [(d + offset, d) for d in range(devices) if 0 <= d + offset < devices]
    return lax.ppermute(value, axis, pairs)


def extended_2(value, sides, width):
    for axis, dim in sides:
        devices, length = (lax.axis_size(axis), value.shape[dim])
        up = [(i, (i + 1) % devices) for i in range(devices - 1)]
        down = [(j, i) for i, j in up]
        last = lax.slice_in_dim(value, length - width, length, axis=dim)
        first = lax.slice_in_dim(value, 0, width, axis=dim)
        before = lax.ppermute(last, axis, up)
        after = lax.ppermute(first, axis, down)
        value = jnp.concatenate([before, value, after], axis=dim)
    return value


def substep(fields, sound_factor, courant, east_edge, west_edge):
    pressure = fields[0]
    zonal_wind = fields[1]
    merid_wind = fields[2]
    east_side = jnp.concatenate([pressure[..., 1:], east_edge[..., None]], axis=-1)
    zonal_next = zonal_wind - courant * (east_side - pressure)
    below_side = jnp.concatenate(
        [pressure[..., 1:, :], jnp.zeros_like(pressure[..., :1, :])], axis=-2
    )
    merid_next = merid_wind - courant * (below_side - pressure)
    west_side = jnp.concatenate([west_edge[..., None], zonal_next[..., :-1]], axis=-1)
    above_side = jnp.concatenate(
        [jnp.zeros_like(merid_next[..., :1, :]), merid_next[..., :-1, :]], axis=-2
    )
    pressure_next = pressure - courant * sound_factor * (
        zonal_next - west_side + (merid_next - above_side)
    )
    return jnp.stack([pressure_next, zonal_next, merid_next])


def repeat_matrix(small, factor):
    rows = jnp.arange(small, dtype=jnp.int32)[:, None]
    cols = jnp.arange(small * factor, dtype=jnp.int32)[None, :] // factor
    return (rows == cols).astype(jnp.float32)


def rotate(value, options, slab, tiles):
    out = value
    for offset, predicate in options:
        pairs = [(s + (w + offset) % slab, s + w) for s in range(0, tiles, slab) for w in range(slab)]
        out = jnp.where(predicate, lax.ppermute(value, "tile", pairs), out)
    return out


def pick(value, options, tiles):
    out = value
    for offset, predicate in options:
        out = jnp.where(predicate, shift_from(value, "tile", offset, tiles), out)
    return out


def local(parent_state, terrain, nest_state, nest_offsets):
    tiles = lax.axis_size("tile")
    tile_index = lax.axis_index("tile")
    levels = parent_state.shape[1]
    parent_rows = parent_state.shape[2]
    nest_rows = nest_state.shape[3]
    nest_cols = nest_state.shape[4]
    coarse_rows = nest_rows // 3
    coarse_cols = nest_cols // 3
    foot_rows = coarse_rows + 2
    assert parent_rows == 2 * coarse_rows and 2 * levels <= coarse_cols
    band_rows = parent_rows * tiles
    nest_total = nest_rows * tiles
    coarse_total = nest_total // 3
    largest_offset = band_rows - coarse_total - 1
    largest_q = largest_offset // parent_rows
    assert largest_q < 16 and tiles % 8 == 0 and tiles >= 32
    center = 8
    planes = 3 * levels
    half = tiles // 2

    row_offset = nest_offsets[0, 0]
    col_offset = nest_offsets[0, 1]
    q = row_offset // parent_rows
    r = row_offset - q * parent_rows

    nest_fields = nest_state[:, :, 0]
    above3 = shift_from(jnp.moveaxis(nest_fields[:, :, nest_rows - 3 :], 2, 0), "tile", -1, tiles)
    below3 = shift_from(jnp.moveaxis(nest_fields[:, :, :3], 2, 0), "tile", 1, tiles)

    sound_factor = 1.0 - terrain.astype(jnp.float32) / terrain_scale
    halo_fields = parent_state[0:3:2]
    line = ("grp", "tile")
    lines = lax.axis_size(line)
    row_above = shift_from(halo_fields[:, :, parent_rows - 1], line, -1, lines)
    row_below = shift_from(halo_fields[:, :, 0], line, 1, lines)
    padded = jnp.concatenate([row_above[:, :, None], halo_fields, row_below[:, :, None]], axis=2)
    zonal_ext = jnp.pad(parent_state[1], ((0, 0), (1, 1), (0, 0)))
    extended = jnp.stack([padded[0], zonal_ext, padded[1]])
    factor_ext = jnp.pad(sound_factor, ((1, 1), (0, 0)))
    edge_zeros = jnp.zeros((levels, parent_rows + 2), jnp.float32)
    advanced = substep(extended, factor_ext, parent_courant, edge_zeros, edge_zeros)[:, :, 1:-1]

    window = lax.dynamic_slice_in_dim(advanced, col_offset - 1, coarse_cols + 2, axis=3)
    factor_window = lax.dynamic_slice_in_dim(sound_factor, col_offset, coarse_cols, axis=1)
    east_col = window[0, :, :, -1].T
    west_col = window[1, :, :, 0].T
    edge_plane = jnp.concatenate(
        [east_col, west_col, jnp.zeros((parent_rows, coarse_cols - 2 * levels), jnp.float32)], axis=1
    )
    rows_here = jnp.concatenate(
        [
            window[..., 1:-1].reshape(planes, parent_rows, coarse_cols),
            factor_window[None],
            edge_plane[None],
        ],
        axis=0,
    )
    above3, below3, block = lax.optimization_barrier((above3, below3, rows_here))
    low = q & 3
    bit2 = ((q >> 2) & 1) == 1
    bit3 = ((q >> 3) & 1) == 1
    low3 = q & (center - 1)
    slab_pos = tile_index % center
    block = rotate(block, [(1, low == 1), (2, low == 2), (3, low == 3)], center, tiles)
    block = rotate(block, [(4, bit2)], center, tiles)
    carry = (slab_pos + low3 >= center).astype(jnp.int32)
    slab_shift = bit3.astype(jnp.int32) + carry - 1
    block = pick(block, [(-center, slab_shift == -1), (center, slab_shift == 1)], tiles)
    extra = foot_rows - 2
    own_even = lax.ppermute(block, "tile", [(m + center, 2 * m) for m in range(half)])
    last_even = lax.ppermute(
        block[:, parent_rows - 1], "tile", [(m + center - 1, 2 * m) for m in range(half)]
    )
    tail_full = lax.ppermute(block, "tile", [(center + half, tiles - 1)])
    tail_rows = lax.ppermute(
        jnp.transpose(block[:, :extra], (1, 0, 2)), "tile", [(center + half, tiles - 2)]
    )
    own_odd = lax.ppermute(own_even, "tile", [(2 * m, 2 * m + 1) for m in range(half)])
    next_odd = lax.ppermute(own_even, "tile", [(2 * m + 2, 2 * m + 1) for m in range(half - 1)])
    next_odd = jnp.where(tile_index == tiles - 1, tail_full, next_odd)
    first_rows = jnp.transpose(own_even[:, :extra], (1, 0, 2))
    next_even = lax.ppermute(first_rows, "tile", [(2 * m + 2, 2 * m) for m in range(half - 1)])
    next_even = jnp.where(tile_index == tiles - 2, tail_rows, next_even)
    even_rows = jnp.concatenate(
        [last_even[:, None], own_even, jnp.transpose(next_even, (1, 0, 2))], axis=1
    )
    odd_rows = jnp.concatenate([own_odd, next_odd], axis=1)
    footprint = jnp.where(
        tile_index % 2 == 0,
        lax.dynamic_slice_in_dim(even_rows, r, foot_rows, axis=1),
        lax.dynamic_slice_in_dim(odd_rows, r + coarse_rows - 1, foot_rows, axis=1),
    )

    widen = repeat_matrix(coarse_cols, 3)
    heighten = repeat_matrix(foot_rows, 3).T
    inner = jnp.einsum("pic,cj->pij", footprint[: planes + 1], widen, precision=HIGHEST)
    expanded = jnp.einsum("ri,pij->prj", heighten, inner, precision=HIGHEST)
    injected = expanded[:planes].reshape(3, levels, 3 * foot_rows, nest_cols)
    nest_factor = expanded[planes]
    east_rows = jnp.repeat(footprint[planes + 1, :, 0:levels].T, 3, axis=1)
    west_rows = jnp.repeat(footprint[planes + 1, :, levels : 2 * levels].T, 3, axis=1)

    local_rows = jnp.arange(3 * foot_rows, dtype=jnp.int32) - 3
    global_rows = nest_rows * tile_index + local_rows
    outside = ((global_rows < 0) | (global_rows >= nest_total))[None, None, :, None]
    fields = jnp.concatenate(
        [jnp.moveaxis(above3, 0, 2), nest_fields, jnp.moveaxis(below3, 0, 2)], axis=2
    )
    for _ in range(SUBSTEPS):
        fields = jnp.where(outside, injected, fields)
        stepped = substep(fields, nest_factor, nest_courant, east_rows, west_rows)
        fields = stepped + nudge_rate * (injected - stepped)
    new_nest = fields[:, :, 3 : 3 + nest_rows]

    narrow = repeat_matrix(coarse_cols, 3).T
    shorten = repeat_matrix(coarse_rows, 3)
    col_sums = jnp.einsum("plrj,jc->plrc", new_nest, narrow, precision=HIGHEST)
    sums = jnp.einsum("kr,plrc->kplc", shorten, col_sums, precision=HIGHEST)
    means = (sums / 9.0).reshape(coarse_rows, planes, coarse_cols)

    gathered = [
        lax.ppermute(
            means, "tile", [(2 * m + k, m + center) for m in range(half + 1) if 0 <= 2 * m + k < tiles]
        )
        for k in (-2, -1, 0, 1)
    ]
    both = jnp.concatenate(gathered, axis=0)
    back = lax.dynamic_slice_in_dim(both, parent_rows - r, parent_rows, axis=0)
    back_carry = carry
    back_shift = bit3.astype(jnp.int32) + back_carry - 1
    back = pick(back, [(-center, back_shift == 1), (center, back_shift == -1)], tiles)
    back = rotate(back, [(-1, low == 1), (-2, low == 2), (-3, low == 3)], center, tiles)
    back = rotate(back, [(-4, bit2)], center, tiles)
    placed = jnp.transpose(back, (1, 0, 2)).reshape(3, levels, parent_rows, coarse_cols)
    band_row = parent_rows * tile_index + jnp.arange(parent_rows, dtype=jnp.int32) - row_offset
    covered = ((band_row >= 0) & (band_row < coarse_total))[None, None, :, None]
    previous = lax.dynamic_slice_in_dim(advanced, col_offset, coarse_cols, axis=3)
    merged = jnp.where(covered, placed, previous)
    new_parent = lax.dynamic_update_slice_in_dim(advanced, merged, col_offset, axis=3)
    return (new_parent, new_nest[:, :, None])


def solution(mesh):
    placed = (
        P(None, None, ("grp", "tile"), None),
        P(("grp", "tile"), None),
        P(None, None, "grp", "tile", None),
        P("grp", None),
    )
    return jax.shard_map(
        local,
        mesh=mesh,
        in_specs=placed,
        out_specs=(P(None, None, ("grp", "tile"), None), P(None, None, "grp", "tile", None)),
        check_vma=False,
    )
```

```python
import jax
import jax.numpy as jnp
from jax import lax
from jax.sharding import PartitionSpec as P

SUBSTEPS = 3


parent_courant = 0.35
nest_courant = 0.35
nudge_rate = 0.2
terrain_scale = 6000.0

HIGHEST = lax.Precision.HIGHEST


def shift_from(value, axis, offset, devices):
    pairs = [(d + offset, d) for d in range(devices) if 0 <= d + offset < devices]
    return lax.ppermute(value, axis, pairs)


def extended_2(value, sides, width):
    for axis, dim in sides:
        devices, length = (lax.axis_size(axis), value.shape[dim])
        up = [(i, (i + 1) % devices) for i in range(devices - 1)]
        down = [(j, i) for i, j in up]
        last = lax.slice_in_dim(value, length - width, length, axis=dim)
        first = lax.slice_in_dim(value, 0, width, axis=dim)
        before = lax.ppermute(last, axis, up)
        after = lax.ppermute(first, axis, down)
        value = jnp.concatenate([before, value, after], axis=dim)
    return value


def substep(fields, sound_factor, courant, east_edge, west_edge):
    pressure = fields[0]
    zonal_wind = fields[1]
    merid_wind = fields[2]
    east_side = jnp.concatenate([pressure[..., 1:], east_edge[..., None]], axis=-1)
    zonal_next = zonal_wind - courant * (east_side - pressure)
    below_side = jnp.concatenate(
        [pressure[..., 1:, :], jnp.zeros_like(pressure[..., :1, :])], axis=-2
    )
    merid_next = merid_wind - courant * (below_side - pressure)
    west_side = jnp.concatenate([west_edge[..., None], zonal_next[..., :-1]], axis=-1)
    above_side = jnp.concatenate(
        [jnp.zeros_like(merid_next[..., :1, :]), merid_next[..., :-1, :]], axis=-2
    )
    pressure_next = pressure - courant * sound_factor * (
        zonal_next - west_side + (merid_next - above_side)
    )
    return jnp.stack([pressure_next, zonal_next, merid_next])


def repeat_matrix(small, factor):
    rows = jnp.arange(small, dtype=jnp.int32)[:, None]
    cols = jnp.arange(small * factor, dtype=jnp.int32)[None, :] // factor
    return (rows == cols).astype(jnp.float32)


def rotate(value, options, slab, tiles):
    out = value
    for offset, predicate in options:
        pairs = [(s + (w + offset) % slab, s + w) for s in range(0, tiles, slab) for w in range(slab)]
        out = jnp.where(predicate, lax.ppermute(value, "tile", pairs), out)
    return out


def pick(value, options, tiles):
    out = value
    for offset, predicate in options:
        out = jnp.where(predicate, shift_from(value, "tile", offset, tiles), out)
    return out


def local(parent_state, terrain, nest_state, nest_offsets):
    tiles = lax.axis_size("tile")
    tile_index = lax.axis_index("tile")
    levels = parent_state.shape[1]
    parent_rows = parent_state.shape[2]
    nest_rows = nest_state.shape[3]
    nest_cols = nest_state.shape[4]
    coarse_rows = nest_rows // 3
    coarse_cols = nest_cols // 3
    foot_rows = coarse_rows + 2
    assert parent_rows == 2 * coarse_rows and 2 * levels <= coarse_cols
    band_rows = parent_rows * tiles
    nest_total = nest_rows * tiles
    coarse_total = nest_total // 3
    largest_offset = band_rows - coarse_total - 1
    largest_q = largest_offset // parent_rows
    assert largest_q < 16 and tiles % 8 == 0 and tiles >= 32
    center = 8
    planes = 3 * levels
    half = tiles // 2

    row_offset = nest_offsets[0, 0]
    col_offset = nest_offsets[0, 1]
    q = row_offset // parent_rows
    r = row_offset - q * parent_rows

    nest_fields = nest_state[:, :, 0]
    above3 = shift_from(jnp.moveaxis(nest_fields[:, :, nest_rows - 3 :], 2, 0), "tile", -1, tiles)
    below3 = shift_from(jnp.moveaxis(nest_fields[:, :, :3], 2, 0), "tile", 1, tiles)

    sound_factor = 1.0 - terrain.astype(jnp.float32) / terrain_scale
    halo_fields = parent_state[0:3:2]
    line = ("grp", "tile")
    lines = lax.axis_size(line)
    row_above = shift_from(halo_fields[:, :, parent_rows - 1], line, -1, lines)
    row_below = shift_from(halo_fields[:, :, 0], line, 1, lines)
    padded = jnp.concatenate([row_above[:, :, None], halo_fields, row_below[:, :, None]], axis=2)
    zonal_ext = jnp.pad(parent_state[1], ((0, 0), (1, 1), (0, 0)))
    extended = jnp.stack([padded[0], zonal_ext, padded[1]])
    factor_ext = jnp.pad(sound_factor, ((1, 1), (0, 0)))
    edge_zeros = jnp.zeros((levels, parent_rows + 2), jnp.float32)
    advanced = substep(extended, factor_ext, parent_courant, edge_zeros, edge_zeros)[:, :, 1:-1]

    window = lax.dynamic_slice_in_dim(advanced, col_offset - 1, coarse_cols + 2, axis=3)
    factor_window = lax.dynamic_slice_in_dim(sound_factor, col_offset, coarse_cols, axis=1)
    east_col = window[0, :, :, -1].T
    west_col = window[1, :, :, 0].T
    edge_plane = jnp.concatenate(
        [east_col, west_col, jnp.zeros((parent_rows, coarse_cols - 2 * levels), jnp.float32)], axis=1
    )
    rows_here = jnp.concatenate(
        [
            window[..., 1:-1].reshape(planes, parent_rows, coarse_cols),
            factor_window[None],
            edge_plane[None],
        ],
        axis=0,
    )
    above3, below3, block = lax.optimization_barrier((above3, below3, rows_here))
    low = q & 3
    bit2 = ((q >> 2) & 1) == 1
    bit3 = ((q >> 3) & 1) == 1
    low3 = q & (center - 1)
    slab_pos = tile_index % center
    block = rotate(block, [(1, low == 1), (2, low == 2), (3, low == 3)], center, tiles)
    block = rotate(block, [(4, bit2)], center, tiles)
    carry = (slab_pos + low3 >= center).astype(jnp.int32)
    slab_shift = bit3.astype(jnp.int32) + carry - 1

    def shift_of(position):
        return bit3.astype(jnp.int32) + (position % center + low3 >= center).astype(jnp.int32) - 1

    def spread(value, first, targets):
        own = first + tile_index // 2
        out = jnp.zeros_like(value)
        for s in (-1, 0, 1):
            pairs = [
                (first + m + center * s, targets(m))
                for m in range(half)
                if 0 <= first + m + center * s < tiles
            ]
            out = jnp.where(shift_of(own) == s, lax.ppermute(value, "tile", pairs), out)
        return out

    extra = foot_rows - 2
    own_even = spread(block, center, lambda m: 2 * m)
    last_even = spread(block[:, parent_rows - 1], center - 1, lambda m: 2 * m)
    next_odd = spread(block, center + 1, lambda m: 2 * m + 1)
    own_odd = lax.ppermute(own_even, "tile", [(2 * m, 2 * m + 1) for m in range(half)])
    first_rows = jnp.transpose(next_odd[:, :extra], (1, 0, 2))
    next_even = lax.ppermute(first_rows, "tile", [(2 * m + 1, 2 * m) for m in range(half)])
    even_rows = jnp.concatenate(
        [last_even[:, None], own_even, jnp.transpose(next_even, (1, 0, 2))], axis=1
    )
    odd_rows = jnp.concatenate([own_odd, next_odd], axis=1)
    footprint = jnp.where(
        tile_index % 2 == 0,
        lax.dynamic_slice_in_dim(even_rows, r, foot_rows, axis=1),
        lax.dynamic_slice_in_dim(odd_rows, r + coarse_rows - 1, foot_rows, axis=1),
    )

    widen = repeat_matrix(coarse_cols, 3)
    heighten = repeat_matrix(foot_rows, 3).T
    inner = jnp.einsum("pic,cj->pij", footprint[: planes + 1], widen, precision=HIGHEST)
    expanded = jnp.einsum("ri,pij->prj", heighten, inner, precision=HIGHEST)
    injected = expanded[:planes].reshape(3, levels, 3 * foot_rows, nest_cols)
    nest_factor = expanded[planes]
    east_rows = jnp.repeat(footprint[planes + 1, :, 0:levels].T, 3, axis=1)
    west_rows = jnp.repeat(footprint[planes + 1, :, levels : 2 * levels].T, 3, axis=1)

    local_rows = jnp.arange(3 * foot_rows, dtype=jnp.int32) - 3
    global_rows = nest_rows * tile_index + local_rows
    outside = ((global_rows < 0) | (global_rows >= nest_total))[None, None, :, None]
    fields = jnp.concatenate(
        [jnp.moveaxis(above3, 0, 2), nest_fields, jnp.moveaxis(below3, 0, 2)], axis=2
    )
    for _ in range(SUBSTEPS):
        fields = jnp.where(outside, injected, fields)
        stepped = substep(fields, nest_factor, nest_courant, east_rows, west_rows)
        fields = stepped + nudge_rate * (injected - stepped)
    new_nest = fields[:, :, 3 : 3 + nest_rows]

    narrow = repeat_matrix(coarse_cols, 3).T
    shorten = repeat_matrix(coarse_rows, 3)
    col_sums = jnp.einsum("plrj,jc->plrc", new_nest, narrow, precision=HIGHEST)
    sums = jnp.einsum("kr,plrc->kplc", shorten, col_sums, precision=HIGHEST)
    means = (sums / 9.0).reshape(coarse_rows, planes, coarse_cols)

    gathered = [
        lax.ppermute(
            means, "tile", [(2 * m + k, m + center) for m in range(half + 1) if 0 <= 2 * m + k < tiles]
        )
        for k in (-2, -1, 0, 1)
    ]
    both = jnp.concatenate(gathered, axis=0)
    back = lax.dynamic_slice_in_dim(both, parent_rows - r, parent_rows, axis=0)
    back_carry = carry
    back_shift = bit3.astype(jnp.int32) + back_carry - 1
    back = pick(back, [(-center, back_shift == 1), (center, back_shift == -1)], tiles)
    back = rotate(back, [(-1, low == 1), (-2, low == 2), (-3, low == 3)], center, tiles)
    back = rotate(back, [(-4, bit2)], center, tiles)
    placed = jnp.transpose(back, (1, 0, 2)).reshape(3, levels, parent_rows, coarse_cols)
    band_row = parent_rows * tile_index + jnp.arange(parent_rows, dtype=jnp.int32) - row_offset
    covered = ((band_row >= 0) & (band_row < coarse_total))[None, None, :, None]
    previous = lax.dynamic_slice_in_dim(advanced, col_offset, coarse_cols, axis=3)
    merged = jnp.where(covered, placed, previous)
    new_parent = lax.dynamic_update_slice_in_dim(advanced, merged, col_offset, axis=3)
    return (new_parent, new_nest[:, :, None])


def solution(mesh):
    placed = (
        P(None, None, ("grp", "tile"), None),
        P(("grp", "tile"), None),
        P(None, None, "grp", "tile", None),
        P("grp", None),
    )
    return jax.shard_map(
        local,
        mesh=mesh,
        in_specs=placed,
        out_specs=(P(None, None, ("grp", "tile"), None), P(None, None, "grp", "tile", None)),
        check_vma=False,
    )
```

```python
import jax
import jax.numpy as jnp
from jax import lax
from jax.sharding import PartitionSpec as P

SUBSTEPS = 3


parent_courant = 0.35
nest_courant = 0.35
nudge_rate = 0.2
terrain_scale = 6000.0

HIGHEST = lax.Precision.HIGHEST


def shift_from(value, axis, offset, devices):
    pairs = [(d + offset, d) for d in range(devices) if 0 <= d + offset < devices]
    return lax.ppermute(value, axis, pairs)


def extended_2(value, sides, width):
    for axis, dim in sides:
        devices, length = (lax.axis_size(axis), value.shape[dim])
        up = [(i, (i + 1) % devices) for i in range(devices - 1)]
        down = [(j, i) for i, j in up]
        last = lax.slice_in_dim(value, length - width, length, axis=dim)
        first = lax.slice_in_dim(value, 0, width, axis=dim)
        before = lax.ppermute(last, axis, up)
        after = lax.ppermute(first, axis, down)
        value = jnp.concatenate([before, value, after], axis=dim)
    return value


def substep(fields, sound_factor, courant, east_edge, west_edge):
    pressure = fields[0]
    zonal_wind = fields[1]
    merid_wind = fields[2]
    east_side = jnp.concatenate([pressure[..., 1:], east_edge[..., None]], axis=-1)
    zonal_next = zonal_wind - courant * (east_side - pressure)
    below_side = jnp.concatenate(
        [pressure[..., 1:, :], jnp.zeros_like(pressure[..., :1, :])], axis=-2
    )
    merid_next = merid_wind - courant * (below_side - pressure)
    west_side = jnp.concatenate([west_edge[..., None], zonal_next[..., :-1]], axis=-1)
    above_side = jnp.concatenate(
        [jnp.zeros_like(merid_next[..., :1, :]), merid_next[..., :-1, :]], axis=-2
    )
    pressure_next = pressure - courant * sound_factor * (
        zonal_next - west_side + (merid_next - above_side)
    )
    return jnp.stack([pressure_next, zonal_next, merid_next])


def repeat_matrix(small, factor):
    rows = jnp.arange(small, dtype=jnp.int32)[:, None]
    cols = jnp.arange(small * factor, dtype=jnp.int32)[None, :] // factor
    return (rows == cols).astype(jnp.float32)


def rotate(value, options, slab, tiles):
    out = value
    for offset, predicate in options:
        pairs = [(s + (w + offset) % slab, s + w) for s in range(0, tiles, slab) for w in range(slab)]
        out = jnp.where(predicate, lax.ppermute(value, "tile", pairs), out)
    return out


def pick(value, options, tiles):
    out = value
    for offset, predicate in options:
        out = jnp.where(predicate, shift_from(value, "tile", offset, tiles), out)
    return out


def local(parent_state, terrain, nest_state, nest_offsets):
    tiles = lax.axis_size("tile")
    tile_index = lax.axis_index("tile")
    levels = parent_state.shape[1]
    parent_rows = parent_state.shape[2]
    nest_rows = nest_state.shape[3]
    nest_cols = nest_state.shape[4]
    coarse_rows = nest_rows // 3
    coarse_cols = nest_cols // 3
    foot_rows = coarse_rows + 2
    assert parent_rows == 2 * coarse_rows and 2 * levels <= coarse_cols
    band_rows = parent_rows * tiles
    nest_total = nest_rows * tiles
    coarse_total = nest_total // 3
    largest_offset = band_rows - coarse_total - 1
    largest_q = largest_offset // parent_rows
    assert largest_q < 16 and tiles % 8 == 0 and tiles >= 32
    center = 8
    planes = 3 * levels
    half = tiles // 2

    row_offset = nest_offsets[0, 0]
    col_offset = nest_offsets[0, 1]
    q = row_offset // parent_rows
    r = row_offset - q * parent_rows

    nest_fields = nest_state[:, :, 0]
    above3 = shift_from(jnp.moveaxis(nest_fields[:, :, nest_rows - 3 :], 2, 0), "tile", -1, tiles)
    below3 = shift_from(jnp.moveaxis(nest_fields[:, :, :3], 2, 0), "tile", 1, tiles)

    sound_factor = 1.0 - terrain.astype(jnp.float32) / terrain_scale
    halo_fields = parent_state[0:3:2]
    line = ("grp", "tile")
    lines = lax.axis_size(line)
    row_above = shift_from(halo_fields[:, :, parent_rows - 1], line, -1, lines)
    row_below = shift_from(halo_fields[:, :, 0], line, 1, lines)
    padded = jnp.concatenate([row_above[:, :, None], halo_fields, row_below[:, :, None]], axis=2)
    zonal_ext = jnp.pad(parent_state[1], ((0, 0), (1, 1), (0, 0)))
    extended = jnp.stack([padded[0], zonal_ext, padded[1]])
    factor_ext = jnp.pad(sound_factor, ((1, 1), (0, 0)))
    edge_zeros = jnp.zeros((levels, parent_rows + 2), jnp.float32)
    advanced = substep(extended, factor_ext, parent_courant, edge_zeros, edge_zeros)[:, :, 1:-1]

    window = lax.dynamic_slice_in_dim(advanced, col_offset - 1, coarse_cols + 2, axis=3)
    factor_window = lax.dynamic_slice_in_dim(sound_factor, col_offset, coarse_cols, axis=1)
    east_col = window[0, :, :, -1].T
    west_col = window[1, :, :, 0].T
    edge_plane = jnp.concatenate(
        [east_col, west_col, jnp.zeros((parent_rows, coarse_cols - 2 * levels), jnp.float32)], axis=1
    )
    rows_here = jnp.concatenate(
        [
            window[..., 1:-1].reshape(planes, parent_rows, coarse_cols),
            factor_window[None],
            edge_plane[None],
        ],
        axis=0,
    )
    above3, below3, block = lax.optimization_barrier((above3, below3, rows_here))
    low = q & 3
    bit2 = ((q >> 2) & 1) == 1
    bit3 = ((q >> 3) & 1) == 1
    low3 = q & (center - 1)
    slab_pos = tile_index % center
    block = rotate(block, [(1, low == 1), (2, low == 2), (3, low == 3)], center, tiles)
    block = rotate(block, [(4, bit2)], center, tiles)
    carry = (slab_pos + low3 >= center).astype(jnp.int32)
    slab_shift = bit3.astype(jnp.int32) + carry - 1
    block = pick(block, [(-center, slab_shift == -1), (center, slab_shift == 1)], tiles)
    extra = foot_rows - 2
    own_even = lax.ppermute(block, "tile", [(m + center, 2 * m) for m in range(half)])
    last_even = lax.ppermute(
        block[:, parent_rows - 1], "tile", [(m + center - 1, 2 * m) for m in range(half)]
    )
    next_odd = lax.ppermute(block, "tile", [(m + center + 1, 2 * m + 1) for m in range(half)])
    own_odd = lax.ppermute(own_even, "tile", [(2 * m, 2 * m + 1) for m in range(half)])
    first_rows = jnp.transpose(next_odd[:, :extra], (1, 0, 2))
    next_even = lax.ppermute(first_rows, "tile", [(2 * m + 1, 2 * m) for m in range(half)])
    even_rows = jnp.concatenate(
        [last_even[:, None], own_even, jnp.transpose(next_even, (1, 0, 2))], axis=1
    )
    odd_rows = jnp.concatenate([own_odd, next_odd], axis=1)
    footprint = jnp.where(
        tile_index % 2 == 0,
        lax.dynamic_slice_in_dim(even_rows, r, foot_rows, axis=1),
        lax.dynamic_slice_in_dim(odd_rows, r + coarse_rows - 1, foot_rows, axis=1),
    )

    widen = repeat_matrix(coarse_cols, 3)
    heighten = repeat_matrix(foot_rows, 3).T
    inner = jnp.einsum("pic,cj->pij", footprint[: planes + 1], widen, precision=HIGHEST)
    expanded = jnp.einsum("ri,pij->prj", heighten, inner, precision=HIGHEST)
    injected = expanded[:planes].reshape(3, levels, 3 * foot_rows, nest_cols)
    nest_factor = expanded[planes]
    east_rows = jnp.repeat(footprint[planes + 1, :, 0:levels].T, 3, axis=1)
    west_rows = jnp.repeat(footprint[planes + 1, :, levels : 2 * levels].T, 3, axis=1)

    local_rows = jnp.arange(3 * foot_rows, dtype=jnp.int32) - 3
    global_rows = nest_rows * tile_index + local_rows
    outside = ((global_rows < 0) | (global_rows >= nest_total))[None, None, :, None]
    fields = jnp.concatenate(
        [jnp.moveaxis(above3, 0, 2), nest_fields, jnp.moveaxis(below3, 0, 2)], axis=2
    )
    for _ in range(SUBSTEPS):
        fields = jnp.where(outside, injected, fields)
        stepped = substep(fields, nest_factor, nest_courant, east_rows, west_rows)
        fields = stepped + nudge_rate * (injected - stepped)
    new_nest = fields[:, :, 3 : 3 + nest_rows]

    narrow = repeat_matrix(coarse_cols, 3).T
    shorten = repeat_matrix(coarse_rows, 3)
    col_sums = jnp.einsum("plrj,jc->plrc", new_nest, narrow, precision=HIGHEST)
    sums = jnp.einsum("kr,plrc->kplc", shorten, col_sums, precision=HIGHEST)
    means = (sums / 9.0).reshape(coarse_rows, planes, coarse_cols)

    gathered = [
        lax.ppermute(
            means, "tile", [(2 * m + k, m + center) for m in range(half + 1) if 0 <= 2 * m + k < tiles]
        )
        for k in (-2, -1, 0, 1)
    ]
    both = jnp.concatenate(gathered, axis=0)
    back = lax.dynamic_slice_in_dim(both, parent_rows - r, parent_rows, axis=0)
    back_carry = carry
    back_shift = bit3.astype(jnp.int32) + back_carry - 1
    back = pick(back, [(-center, back_shift == 1), (center, back_shift == -1)], tiles)
    back = rotate(back, [(-1, (low & 1) == 1)], center, tiles)
    back = rotate(back, [(-2, (low & 2) == 2)], center, tiles)
    back = rotate(back, [(-4, bit2)], center, tiles)
    placed = jnp.transpose(back, (1, 0, 2)).reshape(3, levels, parent_rows, coarse_cols)
    band_row = parent_rows * tile_index + jnp.arange(parent_rows, dtype=jnp.int32) - row_offset
    covered = ((band_row >= 0) & (band_row < coarse_total))[None, None, :, None]
    previous = lax.dynamic_slice_in_dim(advanced, col_offset, coarse_cols, axis=3)
    merged = jnp.where(covered, placed, previous)
    new_parent = lax.dynamic_update_slice_in_dim(advanced, merged, col_offset, axis=3)
    return (new_parent, new_nest[:, :, None])


def solution(mesh):
    placed = (
        P(None, None, ("grp", "tile"), None),
        P(("grp", "tile"), None),
        P(None, None, "grp", "tile", None),
        P("grp", None),
    )
    return jax.shard_map(
        local,
        mesh=mesh,
        in_specs=placed,
        out_specs=(P(None, None, ("grp", "tile"), None), P(None, None, "grp", "tile", None)),
        check_vma=False,
    )
```

```python
import jax
import jax.numpy as jnp
from jax import lax
from jax.sharding import PartitionSpec as P

SUBSTEPS = 3


parent_courant = 0.35
nest_courant = 0.35
nudge_rate = 0.2
terrain_scale = 6000.0

HIGHEST = lax.Precision.HIGHEST


def shift_from(value, axis, offset, devices):
    pairs = [(d + offset, d) for d in range(devices) if 0 <= d + offset < devices]
    return lax.ppermute(value, axis, pairs)


def extended_2(value, sides, width):
    for axis, dim in sides:
        devices, length = (lax.axis_size(axis), value.shape[dim])
        up = [(i, (i + 1) % devices) for i in range(devices - 1)]
        down = [(j, i) for i, j in up]
        last = lax.slice_in_dim(value, length - width, length, axis=dim)
        first = lax.slice_in_dim(value, 0, width, axis=dim)
        before = lax.ppermute(last, axis, up)
        after = lax.ppermute(first, axis, down)
        value = jnp.concatenate([before, value, after], axis=dim)
    return value


def substep(fields, sound_factor, courant, east_edge, west_edge):
    pressure = fields[0]
    zonal_wind = fields[1]
    merid_wind = fields[2]
    east_side = jnp.concatenate([pressure[..., 1:], east_edge[..., None]], axis=-1)
    zonal_next = zonal_wind - courant * (east_side - pressure)
    below_side = jnp.concatenate(
        [pressure[..., 1:, :], jnp.zeros_like(pressure[..., :1, :])], axis=-2
    )
    merid_next = merid_wind - courant * (below_side - pressure)
    west_side = jnp.concatenate([west_edge[..., None], zonal_next[..., :-1]], axis=-1)
    above_side = jnp.concatenate(
        [jnp.zeros_like(merid_next[..., :1, :]), merid_next[..., :-1, :]], axis=-2
    )
    pressure_next = pressure - courant * sound_factor * (
        zonal_next - west_side + (merid_next - above_side)
    )
    return jnp.stack([pressure_next, zonal_next, merid_next])


def repeat_matrix(small, factor):
    rows = jnp.arange(small, dtype=jnp.int32)[:, None]
    cols = jnp.arange(small * factor, dtype=jnp.int32)[None, :] // factor
    return (rows == cols).astype(jnp.float32)


def rotate(value, options, slab, tiles):
    out = value
    for offset, predicate in options:
        pairs = [(s + (w + offset) % slab, s + w) for s in range(0, tiles, slab) for w in range(slab)]
        out = jnp.where(predicate, lax.ppermute(value, "tile", pairs), out)
    return out


def pick(value, options, tiles):
    out = value
    for offset, predicate in options:
        out = jnp.where(predicate, shift_from(value, "tile", offset, tiles), out)
    return out


def local(parent_state, terrain, nest_state, nest_offsets):
    tiles = lax.axis_size("tile")
    tile_index = lax.axis_index("tile")
    levels = parent_state.shape[1]
    parent_rows = parent_state.shape[2]
    nest_rows = nest_state.shape[3]
    nest_cols = nest_state.shape[4]
    coarse_rows = nest_rows // 3
    coarse_cols = nest_cols // 3
    foot_rows = coarse_rows + 2
    assert parent_rows == 2 * coarse_rows and 2 * levels <= coarse_cols
    band_rows = parent_rows * tiles
    nest_total = nest_rows * tiles
    coarse_total = nest_total // 3
    largest_offset = band_rows - coarse_total - 1
    largest_q = largest_offset // parent_rows
    assert largest_q < 16 and tiles % 8 == 0 and tiles >= 32
    center = 8
    planes = 3 * levels
    half = tiles // 2

    row_offset = nest_offsets[0, 0]
    col_offset = nest_offsets[0, 1]
    q = row_offset // parent_rows
    r = row_offset - q * parent_rows

    nest_fields = nest_state[:, :, 0]
    above3 = shift_from(jnp.moveaxis(nest_fields[:, :, nest_rows - 3 :], 2, 0), "tile", -1, tiles)
    below3 = shift_from(jnp.moveaxis(nest_fields[:, :, :3], 2, 0), "tile", 1, tiles)

    sound_factor = 1.0 - terrain.astype(jnp.float32) / terrain_scale
    halo_fields = parent_state[0:3:2]
    line = ("grp", "tile")
    lines = lax.axis_size(line)
    row_above = shift_from(halo_fields[:, :, parent_rows - 1], line, -1, lines)
    row_below = shift_from(halo_fields[:, :, 0], line, 1, lines)
    padded = jnp.concatenate([row_above[:, :, None], halo_fields, row_below[:, :, None]], axis=2)
    zonal_ext = jnp.pad(parent_state[1], ((0, 0), (1, 1), (0, 0)))
    extended = jnp.stack([padded[0], zonal_ext, padded[1]])
    factor_ext = jnp.pad(sound_factor, ((1, 1), (0, 0)))
    edge_zeros = jnp.zeros((levels, parent_rows + 2), jnp.float32)
    advanced = substep(extended, factor_ext, parent_courant, edge_zeros, edge_zeros)[:, :, 1:-1]

    window = lax.dynamic_slice_in_dim(advanced, col_offset - 1, coarse_cols + 2, axis=3)
    factor_window = lax.dynamic_slice_in_dim(sound_factor, col_offset, coarse_cols, axis=1)
    east_col = window[0, :, :, -1].T
    west_col = window[1, :, :, 0].T
    edge_plane = jnp.concatenate(
        [east_col, west_col, jnp.zeros((parent_rows, coarse_cols - 2 * levels), jnp.float32)], axis=1
    )
    rows_here = jnp.concatenate(
        [
            window[..., 1:-1].reshape(planes, parent_rows, coarse_cols),
            factor_window[None],
            edge_plane[None],
        ],
        axis=0,
    )
    above3, below3, block = lax.optimization_barrier((above3, below3, rows_here))
    low = q & 3
    bit2 = ((q >> 2) & 1) == 1
    bit3 = ((q >> 3) & 1) == 1
    low3 = q & (center - 1)
    slab_pos = tile_index % center
    block = rotate(block, [(1, (low & 1) == 1)], center, tiles)
    block = rotate(block, [(2, (low & 2) == 2)], center, tiles)
    block = rotate(block, [(4, bit2)], center, tiles)
    carry = (slab_pos + low3 >= center).astype(jnp.int32)
    slab_shift = bit3.astype(jnp.int32) + carry - 1
    block = pick(block, [(-center, slab_shift == -1), (center, slab_shift == 1)], tiles)
    extra = foot_rows - 2
    own_even = lax.ppermute(block, "tile", [(m + center, 2 * m) for m in range(half)])
    last_even = lax.ppermute(
        block[:, parent_rows - 1], "tile", [(m + center - 1, 2 * m) for m in range(half)]
    )
    next_odd = lax.ppermute(block, "tile", [(m + center + 1, 2 * m + 1) for m in range(half)])
    own_odd = lax.ppermute(own_even, "tile", [(2 * m, 2 * m + 1) for m in range(half)])
    first_rows = jnp.transpose(next_odd[:, :extra], (1, 0, 2))
    next_even = lax.ppermute(first_rows, "tile", [(2 * m + 1, 2 * m) for m in range(half)])
    even_rows = jnp.concatenate(
        [last_even[:, None], own_even, jnp.transpose(next_even, (1, 0, 2))], axis=1
    )
    odd_rows = jnp.concatenate([own_odd, next_odd], axis=1)
    footprint = jnp.where(
        tile_index % 2 == 0,
        lax.dynamic_slice_in_dim(even_rows, r, foot_rows, axis=1),
        lax.dynamic_slice_in_dim(odd_rows, r + coarse_rows - 1, foot_rows, axis=1),
    )

    widen = repeat_matrix(coarse_cols, 3)
    heighten = repeat_matrix(foot_rows, 3).T
    inner = jnp.einsum("pic,cj->pij", footprint[: planes + 1], widen, precision=HIGHEST)
    expanded = jnp.einsum("ri,pij->prj", heighten, inner, precision=HIGHEST)
    injected = expanded[:planes].reshape(3, levels, 3 * foot_rows, nest_cols)
    nest_factor = expanded[planes]
    east_rows = jnp.repeat(footprint[planes + 1, :, 0:levels].T, 3, axis=1)
    west_rows = jnp.repeat(footprint[planes + 1, :, levels : 2 * levels].T, 3, axis=1)

    local_rows = jnp.arange(3 * foot_rows, dtype=jnp.int32) - 3
    global_rows = nest_rows * tile_index + local_rows
    outside = ((global_rows < 0) | (global_rows >= nest_total))[None, None, :, None]
    fields = jnp.concatenate(
        [jnp.moveaxis(above3, 0, 2), nest_fields, jnp.moveaxis(below3, 0, 2)], axis=2
    )
    for _ in range(SUBSTEPS):
        fields = jnp.where(outside, injected, fields)
        stepped = substep(fields, nest_factor, nest_courant, east_rows, west_rows)
        fields = stepped + nudge_rate * (injected - stepped)
    new_nest = fields[:, :, 3 : 3 + nest_rows]

    narrow = repeat_matrix(coarse_cols, 3).T
    shorten = repeat_matrix(coarse_rows, 3)
    col_sums = jnp.einsum("plrj,jc->plrc", new_nest, narrow, precision=HIGHEST)
    sums = jnp.einsum("kr,plrc->kplc", shorten, col_sums, precision=HIGHEST)
    means = (sums / 9.0).reshape(coarse_rows, planes, coarse_cols)

    gathered = [
        lax.ppermute(
            means, "tile", [(2 * m + k, m + center) for m in range(half + 1) if 0 <= 2 * m + k < tiles]
        )
        for k in (-2, -1, 0, 1)
    ]
    both = jnp.concatenate(gathered, axis=0)
    back = lax.dynamic_slice_in_dim(both, parent_rows - r, parent_rows, axis=0)
    back_carry = carry
    back_shift = bit3.astype(jnp.int32) + back_carry - 1
    back = pick(back, [(-center, back_shift == 1), (center, back_shift == -1)], tiles)
    back = rotate(back, [(-1, (low & 1) == 1)], center, tiles)
    back = rotate(back, [(-2, (low & 2) == 2)], center, tiles)
    back = rotate(back, [(-4, bit2)], center, tiles)
    placed = jnp.transpose(back, (1, 0, 2)).reshape(3, levels, parent_rows, coarse_cols)
    band_row = parent_rows * tile_index + jnp.arange(parent_rows, dtype=jnp.int32) - row_offset
    covered = ((band_row >= 0) & (band_row < coarse_total))[None, None, :, None]
    previous = lax.dynamic_slice_in_dim(advanced, col_offset, coarse_cols, axis=3)
    merged = jnp.where(covered, placed, previous)
    new_parent = lax.dynamic_update_slice_in_dim(advanced, merged, col_offset, axis=3)
    return (new_parent, new_nest[:, :, None])


def solution(mesh):
    placed = (
        P(None, None, ("grp", "tile"), None),
        P(("grp", "tile"), None),
        P(None, None, "grp", "tile", None),
        P("grp", None),
    )
    return jax.shard_map(
        local,
        mesh=mesh,
        in_specs=placed,
        out_specs=(P(None, None, ("grp", "tile"), None), P(None, None, "grp", "tile", None)),
        check_vma=False,
    )
```
